256 devices in a mesh: cfg: 2 (over core), seq: 32 (over y, z_lo, x), rep: 4 (over z_hi).
Axes of the slice: x: 4, y: 4, z: 8 (z_hi: 4, z_lo: 2; z = z_hi * 2 + z_lo), core: 2. Of those that a mesh axis runs over, the one named last changes fastest.
Arguments:
- image_tokens: float32 [4, 4608, 1536], P('rep', 'seq')
- text_tokens: bfloat16 [2, 4, 160, 1536], P('cfg', 'rep', 'seq'), may hold values from -6 to 6
- mod_image: float32 [2, 4, 3, 1536], P('cfg', 'rep'), may hold values from -4 to 4
- mod_text: float32 [2, 4, 2, 1536], P('cfg', 'rep'), may hold values from -4 to 4
- text_lengths: int32 [2, 4], P('cfg', 'rep'), may hold values from 38 to 154, as said below
- item_group: int32 [4], P('rep'), may hold values from 0 to 3
- item_step: int32 [4], P('rep'), may hold values from 0 to 27
- step_sizes: float32 [28], replicated, may hold values from 0.05 to 0.4
- guide_scales: float32 [4], replicated, may hold values from 1.5 to 7
- qkv_weight: bfloat16 [1536, 2304], P(('cfg', 'seq', 'rep'))
- kv_weight: bfloat16 [1536, 1536], P(('cfg', 'seq', 'rep')), may hold values from -0.15625 to 0.15625
- out_weight: bfloat16 [768, 1536], P(('cfg', 'seq', 'rep')), may hold values from -0.21875 to 0.21875
Outputs:
- next_tokens: float32 [4, 4608, 1536], P('rep', 'seq', 'cfg')
The draws below stay inside these ranges and needn't reach their ends.
Inputs may be any that keep to these rules, and one draw needn't show every extreme that they name: `text_lengths`: text tokens at or beyond the length are padding; some prompt of every draw has 154 valid tokens.
All inputs are finite; a program needn't handle non-finite values.
Results may differ from the reference program's by a relative error of at most 0.0044.
Values may be sent and summed in bfloat16 or wider, within the bound.
No kernel may reach another device: no remote copies, remote signals or barrier semaphores. Data moves between devices by JAX's collectives and lax.ppermute only.
A program may use at most 128 MiB of HBM per device.

```python
import math
import jax
import jax.numpy as jnp
from jax import lax

D = 1536
HEADS = 12
HEAD_DIM = 64
HW = 768
IMG_DEV = 144
IMG = 4608
TXT = 160
VALID = 154
ITEMS = 4
STEPS = 28
GROUPS = 4
N_SEQ = 32


def draw_image_tokens(key, part):
    first = jax.random.fold_in(key, 0)
    return jnp.clip(jax.random.normal(first, (ITEMS, IMG, D), jnp.float32), -6.0, 6.0)


def draw_qkv_weight(key, part):
    first = jax.random.fold_in(key, 0)
    entries = jax.random.normal(first, (D, 3 * HW), jnp.float32) / math.sqrt(D)
    return entries.astype(jnp.bfloat16)


def draw_text_lengths(key, part):
    first, second = jax.random.split(key)
    drawn = jax.random.randint(first, (2 * ITEMS,), VALID // 4, VALID + 1)
    chosen = jax.random.randint(second, (), 0, 2 * ITEMS)
    drawn = jnp.where(jnp.arange(2 * ITEMS, dtype=jnp.int32) == chosen, VALID, drawn)
    return drawn.reshape(2, ITEMS).astype(jnp.int32)


def touch_ends(values, rng, low, top_value):
    index_at = [jax.random.randint(jax.random.fold_in(rng, axis), (), 0, length) for axis, length in enumerate(values.shape)]
    longest = values.shape.index(max(values.shape))
    next_to = index_at[:longest] + [(index_at[longest] + 1) % values.shape[longest]] + index_at[longest + 1:]
    return values.at[tuple(index_at)].set(low).at[tuple(next_to)].set(top_value)


def level_of(rng, shape, pieces, least, largest):
    loudness = 1.0
    for dim, parts in pieces:
        steps = jax.random.uniform(jax.random.fold_in(jax.random.fold_in(rng, 6), dim), (parts,), jnp.float32, least / len(pieces), largest / len(pieces))
        loudness = loudness * jnp.repeat(jnp.exp(steps), shape[dim] // parts).reshape((-1,) + (1,) * (len(shape) - 1 - dim))
    return loudness


def bell_draw(stream_key, extent, spread, limit, cuts=(), kind=jnp.bfloat16):
    gain = level_of(stream_key, extent, cuts, -0.22, 0.18) if cuts else 1.0
    result = jax.random.normal(stream_key, extent, jnp.float32) * spread * gain
    return jnp.minimum(jnp.maximum(result, -limit), limit).astype(kind)


def setup_inputs(seed: int = 0) -> dict:
    arg_keys = jax.random.split(jax.random.key(seed), 13)
    image_tokens = draw_image_tokens(jax.random.fold_in(arg_keys[12], 71), 0)
    text_tokens = bell_draw(arg_keys[1], (2, ITEMS, TXT, D), 1.0, 6.0, ((0, 2), (1, 4), (2, 32)))
    mod_image = bell_draw(arg_keys[2], (2, ITEMS, 3, D), 1.0, 4.0, ((0, 2), (1, 4)), jnp.float32)
    mod_text = bell_draw(arg_keys[3], (2, ITEMS, 2, D), 1.0, 4.0, ((0, 2), (1, 4)), jnp.float32)
    text_lengths = draw_text_lengths(jax.random.fold_in(arg_keys[12], 71), 0)
    item_group = touch_ends(jax.random.randint(arg_keys[5], (ITEMS,), 0, GROUPS), jax.random.fold_in(arg_keys[5], 1), 0, GROUPS - 1).astype(jnp.int32)
    item_step = touch_ends(jax.random.randint(arg_keys[6], (ITEMS,), 0, STEPS), jax.random.fold_in(arg_keys[6], 1), 0, STEPS - 1).astype(jnp.int32)
    step_sizes = jnp.clip(jnp.exp(jax.random.uniform(arg_keys[7], (STEPS,), jnp.float32, math.log(0.05), math.log(0.4))), 0.05, 0.4)
    guide_scales = jnp.clip(jnp.exp(jax.random.uniform(arg_keys[8], (GROUPS,), jnp.float32, math.log(1.5), math.log(7.0))), 1.5, 7.0)
    qkv_weight = draw_qkv_weight(jax.random.fold_in(arg_keys[12], 71), 0)
    kv_weight = bell_draw(arg_keys[10], (D, 2 * HW), D ** -0.5, 0.15625, ((0, 256),))
    out_weight = bell_draw(arg_keys[11], (HW, D), HW ** -0.5, 0.21875, ((0, 256),))
    return dict(image_tokens=image_tokens, text_tokens=text_tokens, mod_image=mod_image, mod_text=mod_text, text_lengths=text_lengths, item_group=item_group, item_step=item_step, step_sizes=step_sizes, guide_scales=guide_scales, qkv_weight=qkv_weight, kv_weight=kv_weight, out_weight=out_weight)


def layer_norm(values):
    row_mean = lax.optimization_barrier(jnp.mean(values, axis=-1, keepdims=True))
    centred = values - row_mean
    row_var = lax.optimization_barrier(jnp.mean(centred * centred, axis=-1, keepdims=True))
    return centred / jnp.sqrt(row_var + 1e-06)

def half_velocity(picture, prompt, mod_one, mod_two, length, qkv_weight, kv_weight, out_weight):
    heads_width = HEADS * HEAD_DIM
    image_mod = (layer_norm(picture) * (1.0 + mod_one[1]) + mod_one[0]).astype(jnp.bfloat16)
    text_mod = (layer_norm(prompt.astype(jnp.float32)) * (1.0 + mod_two[1]) + mod_two[0]).astype(jnp.bfloat16)
    image_qkv = jnp.dot(image_mod, qkv_weight, preferred_element_type=jnp.float32).astype(jnp.bfloat16)
    text_kv = jnp.dot(text_mod, kv_weight, preferred_element_type=jnp.float32).astype(jnp.bfloat16)
    all_keys = jnp.concatenate([image_qkv[:, heads_width:2 * heads_width], text_kv[:, :heads_width]], axis=0)
    all_keys = all_keys.astype(jnp.float32).reshape(IMG + TXT, HEADS, HEAD_DIM)
    all_values = jnp.concatenate([image_qkv[:, 2 * heads_width:], text_kv[:, heads_width:]], axis=0)
    all_values = all_values.astype(jnp.float32).reshape(IMG + TXT, HEADS, HEAD_DIM)
    usable_key = jnp.concatenate([jnp.ones((IMG,), dtype=bool), jnp.arange(TXT, dtype=jnp.int32) < length])
    queries = image_qkv[:, :heads_width].astype(jnp.float32).reshape(N_SEQ, IMG_DEV, HEADS, HEAD_DIM)

    def query_block(rows):
        scores = jnp.einsum('qhd,khd->hqk', rows, all_keys) * 0.125
        scores = jnp.where(usable_key[None, None, :], scores, -1e+30)
        row_max = lax.optimization_barrier(jnp.max(scores, axis=-1, keepdims=True))
        weights_now = jnp.exp(scores - row_max)
        row_total = lax.optimization_barrier(jnp.sum(weights_now, axis=-1))
        rounded = lax.optimization_barrier(weights_now.astype(jnp.bfloat16)).astype(jnp.float32)
        mixed = jnp.einsum('hqk,khd->qhd', rounded, all_values)
        return mixed / jnp.transpose(row_total)[:, :, None]
    attended = lax.map(query_block, queries).reshape(IMG, heads_width).astype(jnp.bfloat16)
    projected = jnp.dot(attended, out_weight, preferred_element_type=jnp.float32)
    return mod_one[2] * projected

def reference(image_tokens, text_tokens, mod_image, mod_text, text_lengths, item_group, item_step, step_sizes, guide_scales, qkv_weight, kv_weight, out_weight):
    outputs = []
    for item_index in range(ITEMS):
        conditional = half_velocity(image_tokens[item_index], text_tokens[0, item_index], mod_image[0, item_index], mod_text[0, item_index], text_lengths[0, item_index], qkv_weight, kv_weight, out_weight)
        unconditional = half_velocity(image_tokens[item_index], text_tokens[1, item_index], mod_image[1, item_index], mod_text[1, item_index], text_lengths[1, item_index], qkv_weight, kv_weight, out_weight)
        guide_scale = jnp.sum(jnp.where(jnp.arange(GROUPS, dtype=jnp.int32) == item_group[item_index], guide_scales, 0.0))
        step_size = jnp.sum(jnp.where(jnp.arange(STEPS, dtype=jnp.int32) == item_step[item_index], step_sizes, 0.0))
        guided = unconditional + guide_scale * (conditional - unconditional)
        outputs.append(image_tokens[item_index] + step_size * guided)
    return jnp.stack(outputs)
```

```python
import jax
import jax.numpy as jnp
from jax import lax
from jax.sharding import PartitionSpec as P

HEADS = 12
HEAD_DIM = 64


def partner_2(x, axis, apart):
    return lax.ppermute(x, axis, [(i, i ^ 1 << apart) for i in range(lax.axis_size(axis))])


def gather_rows(flat, axes):
    for axis in axes:
        flat = lax.all_gather(flat, axis, axis=0)
    return flat.reshape(-1, flat.shape[-1])


def layer_norm(values):
    row_mean = jnp.mean(values, axis=-1, keepdims=True)
    centred = values - row_mean
    row_var = jnp.mean(centred * centred, axis=-1, keepdims=True)
    return centred / jnp.sqrt(row_var + 1e-06)


def per_device(
    image_tokens,
    text_tokens,
    mod_image,
    mod_text,
    text_lengths,
    item_group,
    item_step,
    step_sizes,
    guide_scales,
    qkv_weight,
    kv_weight,
    out_weight,
):
    image_rows = image_tokens.shape[1]
    text_rows = text_tokens.shape[2]
    model_width = image_tokens.shape[2]
    heads_width = HEADS * HEAD_DIM
    picture = image_tokens[0]
    mod_one = mod_image[0, 0]
    mod_two = mod_text[0, 0]
    image_mod = (layer_norm(picture) * (1.0 + mod_one[1]) + mod_one[0]).astype(jnp.bfloat16)
    text_mod = (
        layer_norm(text_tokens[0, 0].astype(jnp.float32)) * (1.0 + mod_two[1]) + mod_two[0]
    ).astype(jnp.bfloat16)
    qkv_size = qkv_weight.size
    joined = gather_rows(
        jnp.concatenate([qkv_weight.reshape(-1), kv_weight.reshape(-1)]), ("rep", "seq", "cfg")
    )
    qkv_full = joined[:, :qkv_size].reshape(-1, qkv_weight.shape[1])
    kv_full = joined[:, qkv_size:].reshape(-1, kv_weight.shape[1])
    qkv_total = jnp.dot(image_mod, qkv_full, preferred_element_type=jnp.float32)
    kv_total = jnp.dot(text_mod, kv_full, preferred_element_type=jnp.float32)
    image_qkv = qkv_total.astype(jnp.bfloat16)
    text_kv = kv_total.astype(jnp.bfloat16)
    all_keys = jnp.concatenate(
        [image_qkv[:, heads_width : 2 * heads_width], text_kv[:, :heads_width]], axis=0
    )
    all_values = jnp.concatenate(
        [image_qkv[:, 2 * heads_width :], text_kv[:, heads_width:]], axis=0
    )
    queries = image_qkv[:, :heads_width].reshape(image_rows, HEADS, HEAD_DIM)
    length = text_lengths[0, 0]
    key_rows = image_rows + text_rows
    both = lax.all_gather(jnp.concatenate([all_keys, all_values], axis=1), "seq", axis=0, tiled=True)
    pieces = (both[:, :heads_width], both[:, heads_width:])
    running_max = jnp.full((HEADS, image_rows), -1e30, jnp.float32)
    piece_rows = pieces[0].shape[0]
    key_part = pieces[0].reshape(piece_rows, HEADS, HEAD_DIM)
    value_part = pieces[1].reshape(piece_rows, HEADS, HEAD_DIM)
    scores = (
        jnp.einsum("qhd,khd->hqk", queries, key_part, preferred_element_type=jnp.float32) * 0.125
    )
    key_index = jnp.arange(piece_rows, dtype=jnp.int32)
    key_owner = key_index // key_rows
    offset = key_index % key_rows
    usable_key = (offset < image_rows) | (key_owner * text_rows + offset - image_rows < length)
    scores = jnp.where(usable_key[None, None, :], scores, -1e30)
    new_max = jnp.maximum(running_max, jnp.max(scores, axis=-1))
    weights_now = jnp.exp(scores - new_max[:, :, None])
    row_total = jnp.sum(weights_now, axis=-1)
    weighted = jnp.einsum(
        "hqk,khd->hqd",
        weights_now.astype(jnp.bfloat16),
        value_part,
        preferred_element_type=jnp.float32,
    )
    running_max, row_total, weighted = (new_max, row_total, weighted)
    attended = (
        jnp.transpose(weighted / row_total[:, :, None], (1, 0, 2))
        .reshape(image_rows, heads_width)
        .astype(jnp.bfloat16)
    )
    projected = jnp.dot(
        attended,
        gather_rows(out_weight.reshape(-1), ("rep", "seq", "cfg")).reshape(-1, out_weight.shape[1]),
        preferred_element_type=jnp.float32,
    )
    velocity = mod_one[2] * projected
    half_width = model_width // 2
    cfg_index = lax.axis_index("cfg")
    guide_scale = jnp.sum(
        jnp.where(
            jnp.arange(guide_scales.shape[0], dtype=jnp.int32) == item_group[0], guide_scales, 0.0
        )
    )
    step_size = jnp.sum(
        jnp.where(jnp.arange(step_sizes.shape[0], dtype=jnp.int32) == item_step[0], step_sizes, 0.0)
    )
    partner = partner_2(velocity.astype(jnp.bfloat16), "cfg", 0).astype(velocity.dtype)
    cond_full = jnp.where(cfg_index == 0, velocity, partner)
    uncond_full = jnp.where(cfg_index == 0, partner, velocity)
    conditional = lax.dynamic_slice_in_dim(cond_full, cfg_index * half_width, half_width, 1)
    unconditional = lax.dynamic_slice_in_dim(uncond_full, cfg_index * half_width, half_width, 1)
    guided = unconditional + guide_scale * (conditional - unconditional)
    base_part = lax.dynamic_slice_in_dim(picture, cfg_index * half_width, half_width, 1)
    return (base_part + step_size * guided)[None]


def solution(mesh):
    placed = (
        P("rep", "seq", None),
        P("cfg", "rep", "seq", None),
        P("cfg", "rep", None, None),
        P("cfg", "rep", None, None),
        P("cfg", "rep"),
        P("rep"),
        P("rep"),
        P(),
        P(),
        P(("cfg", "seq", "rep"), None),
        P(("cfg", "seq", "rep"), None),
        P(("cfg", "seq", "rep"), None),
    )
    return jax.shard_map(
        per_device, mesh=mesh, in_specs=placed, out_specs=P("rep", "seq", "cfg"), check_vma=False
    )
```

```python
import jax
import jax.numpy as jnp
from jax import lax
from jax.sharding import PartitionSpec as P

HEADS = 12
HEAD_DIM = 64


def partner_2(x, axis, apart):
    return lax.ppermute(x, axis, [(i, i ^ 1 << apart) for i in range(lax.axis_size(axis))])


def digit_shift(count, size, stride, step):
    return [
        (i, i + ((i // stride + step) % size - (i // stride) % size) * stride) for i in range(count)
    ]


def ring_gather(x, axis, size, stride, forward=True):
    count = lax.axis_size(axis)

    def send(v, step):
        return lax.ppermute(v, axis, digit_shift(count, size, stride, step))

    if size == 1:
        return x[None]
    if size == 2:
        return jnp.stack([x, send(x, 1)])
    assert size == 4
    from_left = send(x, 1)
    from_right = send(x, -1)
    if forward:
        cut = x.shape[0] // 2
        far = jnp.concatenate([send(from_left[:cut], 1), send(from_right[cut:], -1)])
    else:
        far = send(x, 2)
    return jnp.stack([x, from_right, far, from_left])


def slot_digits(axis, size, stride):
    own = (lax.axis_index(axis) // stride) % size
    return (own + jnp.arange(size, dtype=jnp.int32)) % size


SEQ_X = (4, 1)
SEQ_Z = (2, 4)
SEQ_Y = (4, 8)


def layer_norm(values):
    row_mean = jnp.mean(values, axis=-1, keepdims=True)
    centred = values - row_mean
    row_var = jnp.mean(centred * centred, axis=-1, keepdims=True)
    return centred / jnp.sqrt(row_var + 1e-06)


def per_device(
    image_tokens,
    text_tokens,
    mod_image,
    mod_text,
    text_lengths,
    item_group,
    item_step,
    step_sizes,
    guide_scales,
    qkv_weight,
    kv_weight,
    out_weight,
):
    image_rows = image_tokens.shape[1]
    text_rows = text_tokens.shape[2]
    model_width = image_tokens.shape[2]
    heads_width = HEADS * HEAD_DIM
    picture = image_tokens[0]
    mod_one = mod_image[0, 0]
    mod_two = mod_text[0, 0]

    qkv_size = qkv_weight.size
    kv_size = kv_weight.size
    flat = jnp.concatenate([qkv_weight.reshape(-1), kv_weight.reshape(-1), out_weight.reshape(-1)])
    rep_size = lax.axis_size("rep")
    cfg_size = lax.axis_size("cfg")
    joined = ring_gather(flat, "rep", rep_size, 1, forward=False)
    joined = ring_gather(joined, "seq", *SEQ_X)
    joined = ring_gather(joined, "seq", *SEQ_Z)
    joined = ring_gather(joined, "seq", *SEQ_Y)
    joined = ring_gather(joined, "cfg", cfg_size, 1)
    seq_size = lax.axis_size("seq")
    source = (
        slot_digits("cfg", cfg_size, 1)[:, None, None, None, None] * (seq_size * rep_size)
        + (
            slot_digits("seq", *SEQ_Y)[None, :, None, None, None] * SEQ_Y[1]
            + slot_digits("seq", *SEQ_Z)[None, None, :, None, None] * SEQ_Z[1]
            + slot_digits("seq", *SEQ_X)[None, None, None, :, None] * SEQ_X[1]
        )
        * rep_size
        + slot_digits("rep", rep_size, 1)[None, None, None, None, :]
    ).reshape(-1)
    joined = joined.reshape(source.shape[0], -1)
    qkv_full = joined[:, :qkv_size].reshape(-1, qkv_weight.shape[1])
    kv_full = joined[:, qkv_size : qkv_size + kv_size].reshape(-1, kv_weight.shape[1])
    out_full = joined[:, qkv_size + kv_size :].reshape(-1, out_weight.shape[1])

    def reorder(values, rows):
        columns = (source[:, None] * rows + jnp.arange(rows, dtype=jnp.int32)[None, :]).reshape(-1)
        return jnp.take(values, columns, axis=1)

    image_mod = (layer_norm(picture) * (1.0 + mod_one[1]) + mod_one[0]).astype(jnp.bfloat16)
    text_mod = (
        layer_norm(text_tokens[0, 0].astype(jnp.float32)) * (1.0 + mod_two[1]) + mod_two[0]
    ).astype(jnp.bfloat16)
    feature_rows = qkv_weight.shape[0]
    qkv_total = jnp.dot(
        reorder(image_mod, feature_rows), qkv_full, preferred_element_type=jnp.float32
    )
    kv_total = jnp.dot(reorder(text_mod, feature_rows), kv_full, preferred_element_type=jnp.float32)
    image_qkv = qkv_total.astype(jnp.bfloat16)
    text_kv = kv_total.astype(jnp.bfloat16)
    local_kv = jnp.concatenate(
        [image_qkv[:, heads_width:], text_kv], axis=0
    )
    queries = image_qkv[:, :heads_width].reshape(image_rows, HEADS, HEAD_DIM)
    length = text_lengths[0, 0]
    key_rows = image_rows + text_rows

    cut = key_rows // 2
    half_a = ring_gather(local_kv[:cut], "seq", *SEQ_Z)
    half_a = ring_gather(half_a, "seq", *SEQ_X)
    half_a = ring_gather(half_a, "seq", *SEQ_Y)
    half_b = ring_gather(local_kv[cut:], "seq", *SEQ_Z)
    half_b = ring_gather(half_b, "seq", *SEQ_Y)
    half_b = ring_gather(half_b, "seq", *SEQ_X)
    owner_a = (
        slot_digits("seq", *SEQ_Y)[:, None, None] * SEQ_Y[1]
        + slot_digits("seq", *SEQ_X)[None, :, None] * SEQ_X[1]
        + slot_digits("seq", *SEQ_Z)[None, None, :] * SEQ_Z[1]
    )
    owner_b = (
        slot_digits("seq", *SEQ_X)[:, None, None] * SEQ_X[1]
        + slot_digits("seq", *SEQ_Y)[None, :, None] * SEQ_Y[1]
        + slot_digits("seq", *SEQ_Z)[None, None, :] * SEQ_Z[1]
    )
    owner = jnp.concatenate(
        [
            jnp.broadcast_to(owner_a.reshape(-1, 1), (owner_a.size, cut)).reshape(-1),
            jnp.broadcast_to(owner_b.reshape(-1, 1), (owner_b.size, key_rows - cut)).reshape(-1),
        ]
    )
    offset = jnp.concatenate(
        [
            jnp.broadcast_to(jnp.arange(cut, dtype=jnp.int32), (owner_a.size, cut)).reshape(-1),
            jnp.broadcast_to(
                jnp.arange(cut, key_rows, dtype=jnp.int32), (owner_b.size, key_rows - cut)
            ).reshape(-1),
        ]
    )
    usable_key = (offset < image_rows) | (owner * text_rows + offset - image_rows < length)
    gathered = jnp.concatenate(
        [half_a.reshape(-1, local_kv.shape[1]), half_b.reshape(-1, local_kv.shape[1])], axis=0
    )
    piece_rows = gathered.shape[0]
    key_part = gathered[:, :heads_width].reshape(piece_rows, HEADS, HEAD_DIM)
    value_part = gathered[:, heads_width:].reshape(piece_rows, HEADS, HEAD_DIM)
    scores = (
        jnp.einsum("qhd,khd->hqk", queries, key_part, preferred_element_type=jnp.float32) * 0.125
    )
    scores = jnp.where(usable_key[None, None, :], scores, -1e30)
    row_max = jnp.max(scores, axis=-1)
    weights_now = jnp.exp(scores - row_max[:, :, None])
    row_total = jnp.sum(weights_now, axis=-1)
    weighted = jnp.einsum(
        "hqk,khd->hqd",
        weights_now.astype(jnp.bfloat16),
        value_part,
        preferred_element_type=jnp.float32,
    )
    attended = (
        jnp.transpose(weighted / row_total[:, :, None], (1, 0, 2))
        .reshape(image_rows, heads_width)
        .astype(jnp.bfloat16)
    )
    projected = jnp.dot(
        reorder(attended, out_weight.shape[0]), out_full, preferred_element_type=jnp.float32
    )
    velocity = mod_one[2] * projected
    half_width = model_width // 2
    cfg_index = lax.axis_index("cfg")
    guide_scale = jnp.sum(
        jnp.where(
            jnp.arange(guide_scales.shape[0], dtype=jnp.int32) == item_group[0], guide_scales, 0.0
        )
    )
    step_size = jnp.sum(
        jnp.where(jnp.arange(step_sizes.shape[0], dtype=jnp.int32) == item_step[0], step_sizes, 0.0)
    )
    partner = partner_2(velocity.astype(jnp.bfloat16), "cfg", 0).astype(velocity.dtype)
    cond_full = jnp.where(cfg_index == 0, velocity, partner)
    uncond_full = jnp.where(cfg_index == 0, partner, velocity)
    conditional = lax.dynamic_slice_in_dim(cond_full, cfg_index * half_width, half_width, 1)
    unconditional = lax.dynamic_slice_in_dim(uncond_full, cfg_index * half_width, half_width, 1)
    guided = unconditional + guide_scale * (conditional - unconditional)
    base_part = lax.dynamic_slice_in_dim(picture, cfg_index * half_width, half_width, 1)
    return (base_part + step_size * guided)[None]


def solution(mesh):
    placed = (
        P("rep", "seq", None),
        P("cfg", "rep", "seq", None),
        P("cfg", "rep", None, None),
        P("cfg", "rep", None, None),
        P("cfg", "rep"),
        P("rep"),
        P("rep"),
        P(),
        P(),
        P(("cfg", "seq", "rep"), None),
        P(("cfg", "seq", "rep"), None),
        P(("cfg", "seq", "rep"), None),
    )
    return jax.shard_map(
        per_device, mesh=mesh, in_specs=placed, out_specs=P("rep", "seq", "cfg"), check_vma=False
    )
```

```python
import jax
import jax.numpy as jnp
from jax import lax
from jax.sharding import PartitionSpec as P

HEADS = 12
HEAD_DIM = 64


def partner_2(x, axis, apart):
    return lax.ppermute(x, axis, [(i, i ^ 1 << apart) for i in range(lax.axis_size(axis))])


def digit_shift(count, size, stride, step):
    return [
        (i, i + ((i // stride + step) % size - (i // stride) % size) * stride) for i in range(count)
    ]


def ring_gather(x, axis, size, stride, forward=True):
    count = lax.axis_size(axis)
    tmap = jax.tree.map

    def send(v, step):
        return lax.ppermute(v, axis, digit_shift(count, size, stride, step))

    if size == 1:
        return tmap(lambda v: v[None], x)
    if size == 2:
        return tmap(lambda v, w: jnp.stack([v, w]), x, send(x, 1))
    assert size == 4
    from_left = send(x, 1)
    from_right = send(x, -1)
    if forward:
        head = send(tmap(lambda v: v[: v.shape[0] // 2], from_left), 1)
        tail = send(tmap(lambda v: v[v.shape[0] // 2 :], from_right), -1)
        far = tmap(lambda u, v: jnp.concatenate([u, v]), head, tail)
    else:
        far = send(x, 2)
    return tmap(lambda *vs: jnp.stack(vs), x, from_right, far, from_left)


def slot_digits(axis, size, stride):
    own = (lax.axis_index(axis) // stride) % size
    return (own + jnp.arange(size, dtype=jnp.int32)) % size


SEQ_X = (4, 1)
SEQ_Z = (2, 4)
SEQ_Y = (4, 8)


def layer_norm(values):
    row_mean = jnp.mean(values, axis=-1, keepdims=True)
    centred = values - row_mean
    row_var = jnp.mean(centred * centred, axis=-1, keepdims=True)
    return centred / jnp.sqrt(row_var + 1e-06)


def per_device(
    image_tokens,
    text_tokens,
    mod_image,
    mod_text,
    text_lengths,
    item_group,
    item_step,
    step_sizes,
    guide_scales,
    qkv_weight,
    kv_weight,
    out_weight,
):
    image_rows = image_tokens.shape[1]
    text_rows = text_tokens.shape[2]
    model_width = image_tokens.shape[2]
    heads_width = HEADS * HEAD_DIM
    picture = image_tokens[0]
    mod_one = mod_image[0, 0]
    mod_two = mod_text[0, 0]

    rep_size = lax.axis_size("rep")
    seq_size = lax.axis_size("seq")
    weights = (qkv_weight, kv_weight, out_weight)
    weights = ring_gather(weights, "rep", rep_size, 1, forward=False)
    weights = ring_gather(weights, "seq", *SEQ_X)
    weights = jax.tree.map(lambda w: w.reshape(-1, w.shape[-1]), weights)
    weights = ring_gather(weights, "seq", *SEQ_Z)
    weights = ring_gather(weights, "seq", *SEQ_Y)
    qkv_half, kv_half, out_half = jax.tree.map(lambda w: w.reshape(-1, w.shape[-1]), weights)
    cfg_index = lax.axis_index("cfg")
    source = (
        (
            slot_digits("seq", *SEQ_Y)[:, None, None, None] * SEQ_Y[1]
            + slot_digits("seq", *SEQ_Z)[None, :, None, None] * SEQ_Z[1]
            + slot_digits("seq", *SEQ_X)[None, None, :, None] * SEQ_X[1]
        )
        * rep_size
        + slot_digits("rep", rep_size, 1)[None, None, None, :]
    ).reshape(-1)

    def columns(half, rows):
        owner = half * (seq_size * rep_size) + source
        return (owner[:, None] * rows + jnp.arange(rows, dtype=jnp.int32)[None, :]).reshape(-1)

    mod_other, text_other, mod_text_other = partner_2(
        (mod_one, text_tokens[0, 0], mod_two), "cfg", 0
    )

    def modulate(values, mod):
        return (layer_norm(values.astype(jnp.float32)) * (1.0 + mod[1]) + mod[0]).astype(
            jnp.bfloat16
        )

    image_mod = modulate(picture, mod_one)
    text_mod = modulate(text_tokens[0, 0], mod_two)
    image_other = modulate(picture, mod_other)
    text_other_mod = modulate(text_other, mod_text_other)
    feature_cols = columns(cfg_index, qkv_weight.shape[0])

    def project(values, weight):
        return jnp.dot(
            jnp.take(values, feature_cols, axis=1), weight, preferred_element_type=jnp.float32
        )

    sent = partner_2((project(image_other, qkv_half), project(text_other_mod, kv_half)), "cfg", 0)
    qkv_total = project(image_mod, qkv_half) + sent[0]
    kv_total = project(text_mod, kv_half) + sent[1]
    out_other = partner_2(out_half, "cfg", 0)
    image_qkv = qkv_total.astype(jnp.bfloat16)
    text_kv = kv_total.astype(jnp.bfloat16)
    local_kv = jnp.concatenate(
        [image_qkv[:, heads_width:], text_kv], axis=0
    )
    queries = image_qkv[:, :heads_width].reshape(image_rows, HEADS, HEAD_DIM)
    length = text_lengths[0, 0]
    key_rows = image_rows + text_rows

    cut = key_rows // 2
    half_a = ring_gather(local_kv[:cut], "seq", *SEQ_Z)
    half_a = ring_gather(half_a, "seq", *SEQ_X)
    half_a = ring_gather(half_a, "seq", *SEQ_Y)
    half_b = ring_gather(local_kv[cut:], "seq", *SEQ_Z)
    half_b = ring_gather(half_b, "seq", *SEQ_Y)
    half_b = ring_gather(half_b, "seq", *SEQ_X)
    owner_a = (
        slot_digits("seq", *SEQ_Y)[:, None, None] * SEQ_Y[1]
        + slot_digits("seq", *SEQ_X)[None, :, None] * SEQ_X[1]
        + slot_digits("seq", *SEQ_Z)[None, None, :] * SEQ_Z[1]
    )
    owner_b = (
        slot_digits("seq", *SEQ_X)[:, None, None] * SEQ_X[1]
        + slot_digits("seq", *SEQ_Y)[None, :, None] * SEQ_Y[1]
        + slot_digits("seq", *SEQ_Z)[None, None, :] * SEQ_Z[1]
    )
    owner = jnp.concatenate(
        [
            jnp.broadcast_to(owner_a.reshape(-1, 1), (owner_a.size, cut)).reshape(-1),
            jnp.broadcast_to(owner_b.reshape(-1, 1), (owner_b.size, key_rows - cut)).reshape(-1),
        ]
    )
    offset = jnp.concatenate(
        [
            jnp.broadcast_to(jnp.arange(cut, dtype=jnp.int32), (owner_a.size, cut)).reshape(-1),
            jnp.broadcast_to(
                jnp.arange(cut, key_rows, dtype=jnp.int32), (owner_b.size, key_rows - cut)
            ).reshape(-1),
        ]
    )
    usable_key = (offset < image_rows) | (owner * text_rows + offset - image_rows < length)
    gathered = jnp.concatenate(
        [half_a.reshape(-1, local_kv.shape[1]), half_b.reshape(-1, local_kv.shape[1])], axis=0
    )
    piece_rows = gathered.shape[0]
    key_part = gathered[:, :heads_width].reshape(piece_rows, HEADS, HEAD_DIM)
    value_part = gathered[:, heads_width:].reshape(piece_rows, HEADS, HEAD_DIM)
    scores = (
        jnp.einsum("qhd,khd->hqk", queries, key_part, preferred_element_type=jnp.float32) * 0.125
    )
    scores = jnp.where(usable_key[None, None, :], scores, -1e30)
    row_max = jnp.max(scores, axis=-1)
    weights_now = jnp.exp(scores - row_max[:, :, None])
    row_total = jnp.sum(weights_now, axis=-1)
    weighted = jnp.einsum(
        "hqk,khd->hqd",
        weights_now.astype(jnp.bfloat16),
        value_part,
        preferred_element_type=jnp.float32,
    )
    attended = (
        jnp.transpose(weighted / row_total[:, :, None], (1, 0, 2))
        .reshape(image_rows, heads_width)
        .astype(jnp.bfloat16)
    )
    out_rows = out_weight.shape[0]
    projected = jnp.dot(
        jnp.take(attended, columns(cfg_index, out_rows), axis=1),
        out_half,
        preferred_element_type=jnp.float32,
    ) + jnp.dot(
        jnp.take(attended, columns(1 - cfg_index, out_rows), axis=1),
        out_other,
        preferred_element_type=jnp.float32,
    )
    velocity = mod_one[2] * projected
    half_width = model_width // 2
    guide_scale = jnp.sum(
        jnp.where(
            jnp.arange(guide_scales.shape[0], dtype=jnp.int32) == item_group[0], guide_scales, 0.0
        )
    )
    step_size = jnp.sum(
        jnp.where(jnp.arange(step_sizes.shape[0], dtype=jnp.int32) == item_step[0], step_sizes, 0.0)
    )
    partner = partner_2(velocity.astype(jnp.bfloat16), "cfg", 0).astype(velocity.dtype)
    cond_full = jnp.where(cfg_index == 0, velocity, partner)
    uncond_full = jnp.where(cfg_index == 0, partner, velocity)
    conditional = lax.dynamic_slice_in_dim(cond_full, cfg_index * half_width, half_width, 1)
    unconditional = lax.dynamic_slice_in_dim(uncond_full, cfg_index * half_width, half_width, 1)
    guided = unconditional + guide_scale * (conditional - unconditional)
    base_part = lax.dynamic_slice_in_dim(picture, cfg_index * half_width, half_width, 1)
    return (base_part + step_size * guided)[None]


def solution(mesh):
    placed = (
        P("rep", "seq", None),
        P("cfg", "rep", "seq", None),
        P("cfg", "rep", None, None),
        P("cfg", "rep", None, None),
        P("cfg", "rep"),
        P("rep"),
        P("rep"),
        P(),
        P(),
        P(("cfg", "seq", "rep"), None),
        P(("cfg", "seq", "rep"), None),
        P(("cfg", "seq", "rep"), None),
    )
    return jax.shard_map(
        per_device, mesh=mesh, in_specs=placed, out_specs=P("rep", "seq", "cfg"), check_vma=False
    )
```

```python
import jax
import jax.numpy as jnp
from jax import lax
from jax.sharding import PartitionSpec as P
from jax.experimental import pallas as pl

HEADS = 12
HEAD_DIM = 64


def partner_2(x, axis, apart):
    return lax.ppermute(x, axis, [(i, i ^ 1 << apart) for i in range(lax.axis_size(axis))])


def digit_shift(count, size, stride, step):
    return [
        (i, i + ((i // stride + step) % size - (i // stride) % size) * stride) for i in range(count)
    ]


def ring_gather(x, axis, size, stride, forward=True):
    count = lax.axis_size(axis)
    tmap = jax.tree.map

    def send(v, step):
        return lax.ppermute(v, axis, digit_shift(count, size, stride, step))

    if size == 1:
        return tmap(lambda v: v[None], x)
    if size == 2:
        return tmap(lambda v, w: jnp.stack([v, w]), x, send(x, 1))
    assert size == 4
    from_left = send(x, 1)
    from_right = send(x, -1)
    if forward:
        head = send(tmap(lambda v: v[: v.shape[0] // 2], from_left), 1)
        tail = send(tmap(lambda v: v[v.shape[0] // 2 :], from_right), -1)
        far = tmap(lambda u, v: jnp.concatenate([u, v]), head, tail)
    else:
        far = send(x, 2)
    return tmap(lambda *vs: jnp.stack(vs), x, from_right, far, from_left)


def slot_digits(axis, size, stride):
    own = (lax.axis_index(axis) // stride) % size
    return (own + jnp.arange(size, dtype=jnp.int32)) % size


SEQ_X = (4, 1)
SEQ_Z = (2, 4)
SEQ_Y = (4, 8)


def layer_norm(values):
    row_mean = jnp.mean(values, axis=-1, keepdims=True)
    centred = values - row_mean
    row_var = jnp.mean(centred * centred, axis=-1, keepdims=True)
    return centred / jnp.sqrt(row_var + 1e-06)


def attention_kernel(q_ref, ka_ref, va_ref, kb_ref, vb_ref, kt_ref, vt_ref, valid_ref, o_ref):
    usable = valid_ref[...] > 0.0
    contract = (((1,), (1,)), ((), ()))
    results = []
    for head in range(2):
        lanes = slice(head * HEAD_DIM, (head + 1) * HEAD_DIM)
        query = q_ref[:, lanes]

        def scores(k_ref):
            return (
                lax.dot_general(query, k_ref[:, lanes], contract, preferred_element_type=jnp.float32)
                * 0.125
            )

        s_a = scores(ka_ref)
        s_b = scores(kb_ref)
        s_t = jnp.where(usable, scores(kt_ref), -1e30)
        top = jnp.maximum(
            jnp.maximum(jnp.max(s_a, axis=-1, keepdims=True), jnp.max(s_b, axis=-1, keepdims=True)),
            jnp.max(s_t, axis=-1, keepdims=True),
        )
        total = jnp.zeros((query.shape[0], 1), jnp.float32)
        mixed = jnp.zeros((query.shape[0], HEAD_DIM), jnp.float32)
        for part, v_ref in ((s_a, va_ref), (s_b, vb_ref), (s_t, vt_ref)):
            probs = jnp.exp(part - top)
            total = total + jnp.sum(probs, axis=-1, keepdims=True)
            mixed = mixed + jnp.dot(
                probs.astype(jnp.bfloat16), v_ref[:, lanes], preferred_element_type=jnp.float32
            )
        results.append(mixed / total)
    o_ref[...] = jnp.concatenate(results, axis=1).astype(o_ref.dtype)


def attention(image_qkv, keys_a, keys_b, keys_t, valid):
    rows = image_qkv.shape[0]
    pairs = HEADS // 2
    width = 2 * HEAD_DIM

    def spec(array, offset):
        return pl.BlockSpec((array.shape[0], width), lambda j: (0, j + offset))

    return pl.pallas_call(
        attention_kernel,
        grid=(pairs,),
        in_specs=[
            spec(image_qkv, 0),
            spec(keys_a, 0),
            spec(keys_a, pairs),
            spec(keys_b, 0),
            spec(keys_b, pairs),
            spec(keys_t, 0),
            spec(keys_t, pairs),
            pl.BlockSpec(valid.shape, lambda j: (0, 0)),
        ],
        out_specs=pl.BlockSpec((rows, width), lambda j: (0, j)),
        out_shape=jax.ShapeDtypeStruct((rows, HEADS * HEAD_DIM), jnp.bfloat16),
    )(image_qkv, keys_a, keys_a, keys_b, keys_b, keys_t, keys_t, valid)


def per_device(
    image_tokens,
    text_tokens,
    mod_image,
    mod_text,
    text_lengths,
    item_group,
    item_step,
    step_sizes,
    guide_scales,
    qkv_weight,
    kv_weight,
    out_weight,
):
    image_rows = image_tokens.shape[1]
    text_rows = text_tokens.shape[2]
    model_width = image_tokens.shape[2]
    heads_width = HEADS * HEAD_DIM
    picture = image_tokens[0]
    mod_one = mod_image[0, 0]
    mod_two = mod_text[0, 0]

    rep_size = lax.axis_size("rep")
    seq_size = lax.axis_size("seq")
    weights = (qkv_weight, kv_weight, out_weight)
    weights = ring_gather(weights, "rep", rep_size, 1, forward=False)
    weights = ring_gather(weights, "seq", *SEQ_X)
    weights = jax.tree.map(lambda w: w.reshape(-1, w.shape[-1]), weights)
    weights = ring_gather(weights, "seq", *SEQ_Z)
    weights = ring_gather(weights, "seq", *SEQ_Y)
    qkv_half, kv_half, out_half = jax.tree.map(lambda w: w.reshape(-1, w.shape[-1]), weights)
    cfg_index = lax.axis_index("cfg")
    source = (
        (
            slot_digits("seq", *SEQ_Y)[:, None, None, None] * SEQ_Y[1]
            + slot_digits("seq", *SEQ_Z)[None, :, None, None] * SEQ_Z[1]
            + slot_digits("seq", *SEQ_X)[None, None, :, None] * SEQ_X[1]
        )
        * rep_size
        + slot_digits("rep", rep_size, 1)[None, None, None, :]
    ).reshape(-1)

    def columns(half, rows):
        owner = half * (seq_size * rep_size) + source
        return (owner[:, None] * rows + jnp.arange(rows, dtype=jnp.int32)[None, :]).reshape(-1)

    mod_other, text_other, mod_text_other = partner_2(
        (mod_one, text_tokens[0, 0], mod_two), "cfg", 0
    )

    def modulate(values, mod):
        return (layer_norm(values.astype(jnp.float32)) * (1.0 + mod[1]) + mod[0]).astype(
            jnp.bfloat16
        )

    image_mod = modulate(picture, mod_one)
    text_mod = modulate(text_tokens[0, 0], mod_two)
    image_other = modulate(picture, mod_other)
    text_other_mod = modulate(text_other, mod_text_other)
    feature_cols = columns(cfg_index, qkv_weight.shape[0])

    def project(values, weight):
        return jnp.dot(
            jnp.take(values, feature_cols, axis=1), weight, preferred_element_type=jnp.float32
        )

    sent = partner_2((project(image_other, qkv_half), project(text_other_mod, kv_half)), "cfg", 0)
    qkv_total = project(image_mod, qkv_half) + sent[0]
    kv_total = project(text_mod, kv_half) + sent[1]
    out_other = partner_2(out_half, "cfg", 0)
    image_qkv = qkv_total.astype(jnp.bfloat16)
    text_kv = kv_total.astype(jnp.bfloat16)
    length = text_lengths[0, 0]
    image_kv = image_qkv[:, heads_width:]

    cut = 64
    part_a = (image_kv[:cut], text_kv)
    part_a = ring_gather(part_a, "seq", *SEQ_Z)
    part_a = ring_gather(part_a, "seq", *SEQ_X)
    part_a = ring_gather(part_a, "seq", *SEQ_Y)
    part_b = ring_gather(image_kv[cut:], "seq", *SEQ_Z)
    part_b = ring_gather(part_b, "seq", *SEQ_Y)
    part_b = ring_gather(part_b, "seq", *SEQ_X)
    owner_a = (
        slot_digits("seq", *SEQ_Y)[:, None, None] * SEQ_Y[1]
        + slot_digits("seq", *SEQ_X)[None, :, None] * SEQ_X[1]
        + slot_digits("seq", *SEQ_Z)[None, None, :] * SEQ_Z[1]
    ).reshape(-1)
    position = owner_a[:, None] * text_rows + jnp.arange(text_rows, dtype=jnp.int32)[None, :]
    valid = (position < length).astype(jnp.float32).reshape(1, -1)
    width = image_kv.shape[1]
    attended = attention(
        image_qkv,
        part_a[0].reshape(-1, width),
        part_b.reshape(-1, width),
        part_a[1].reshape(-1, width),
        valid,
    )
    out_rows = out_weight.shape[0]
    projected = jnp.dot(
        jnp.take(attended, columns(cfg_index, out_rows), axis=1),
        out_half,
        preferred_element_type=jnp.float32,
    ) + jnp.dot(
        jnp.take(attended, columns(1 - cfg_index, out_rows), axis=1),
        out_other,
        preferred_element_type=jnp.float32,
    )
    velocity = mod_one[2] * projected
    half_width = model_width // 2
    guide_scale = jnp.sum(
        jnp.where(
            jnp.arange(guide_scales.shape[0], dtype=jnp.int32) == item_group[0], guide_scales, 0.0
        )
    )
    step_size = jnp.sum(
        jnp.where(jnp.arange(step_sizes.shape[0], dtype=jnp.int32) == item_step[0], step_sizes, 0.0)
    )
    partner = partner_2(velocity.astype(jnp.bfloat16), "cfg", 0).astype(velocity.dtype)
    cond_full = jnp.where(cfg_index == 0, velocity, partner)
    uncond_full = jnp.where(cfg_index == 0, partner, velocity)
    conditional = lax.dynamic_slice_in_dim(cond_full, cfg_index * half_width, half_width, 1)
    unconditional = lax.dynamic_slice_in_dim(uncond_full, cfg_index * half_width, half_width, 1)
    guided = unconditional + guide_scale * (conditional - unconditional)
    base_part = lax.dynamic_slice_in_dim(picture, cfg_index * half_width, half_width, 1)
    return (base_part + step_size * guided)[None]


def solution(mesh):
    placed = (
        P("rep", "seq", None),
        P("cfg", "rep", "seq", None),
        P("cfg", "rep", None, None),
        P("cfg", "rep", None, None),
        P("cfg", "rep"),
        P("rep"),
        P("rep"),
        P(),
        P(),
        P(("cfg", "seq", "rep"), None),
        P(("cfg", "seq", "rep"), None),
        P(("cfg", "seq", "rep"), None),
    )
    return jax.shard_map(
        per_device, mesh=mesh, in_specs=placed, out_specs=P("rep", "seq", "cfg"), check_vma=False
    )
```

```python
import jax
import jax.numpy as jnp
from jax import lax
from jax.sharding import PartitionSpec as P
from jax.experimental import pallas as pl

HEADS = 12
HEAD_DIM = 64


def partner_2(x, axis, apart):
    return lax.ppermute(x, axis, [(i, i ^ 1 << apart) for i in range(lax.axis_size(axis))])


def digit_shift(count, size, stride, step):
    return [
        (i, i + ((i // stride + step) % size - (i // stride) % size) * stride) for i in range(count)
    ]


def ring_gather(x, axis, size, stride, forward=True):
    count = lax.axis_size(axis)
    tmap = jax.tree.map

    def send(v, step):
        return lax.ppermute(v, axis, digit_shift(count, size, stride, step))

    if size == 1:
        return tmap(lambda v: v[None], x)
    if size == 2:
        return tmap(lambda v, w: jnp.stack([v, w]), x, send(x, 1))
    assert size == 4
    from_left = send(x, 1)
    from_right = send(x, -1)
    if forward:
        head = send(tmap(lambda v: v[: v.shape[0] // 2], from_left), 1)
        tail = send(tmap(lambda v: v[v.shape[0] // 2 :], from_right), -1)
        far = tmap(lambda u, v: jnp.concatenate([u, v]), head, tail)
    else:
        far = send(x, 2)
    return tmap(lambda *vs: jnp.stack(vs), x, from_right, far, from_left)


def slot_digits(axis, size, stride):
    own = (lax.axis_index(axis) // stride) % size
    return (own + jnp.arange(size, dtype=jnp.int32)) % size


SEQ_X = (4, 1)
SEQ_Z = (2, 4)
SEQ_Y = (4, 8)


def layer_norm(values):
    row_mean = jnp.mean(values, axis=-1, keepdims=True)
    centred = values - row_mean
    row_var = jnp.mean(centred * centred, axis=-1, keepdims=True)
    return centred / jnp.sqrt(row_var + 1e-06)


def attention_kernel(q_ref, ka_ref, va_ref, kb_ref, vb_ref, valid_ref, o_ref):
    usable = valid_ref[...] > 0.0
    contract = (((1,), (1,)), ((), ()))
    results = []
    for head in range(2):
        lanes = slice(head * HEAD_DIM, (head + 1) * HEAD_DIM)
        query = q_ref[:, lanes]

        def scores(k_ref):
            return (
                lax.dot_general(query, k_ref[:, lanes], contract, preferred_element_type=jnp.float32)
                * 0.125
            )

        s_a = jnp.where(usable, scores(ka_ref), -1e30)
        s_b = scores(kb_ref)
        top = jnp.maximum(jnp.max(s_a, axis=-1, keepdims=True), jnp.max(s_b, axis=-1, keepdims=True))
        total = jnp.zeros((query.shape[0], 1), jnp.float32)
        mixed = jnp.zeros((query.shape[0], HEAD_DIM), jnp.float32)
        for part, v_ref in ((s_a, va_ref), (s_b, vb_ref)):
            probs = jnp.exp(part - top)
            total = total + jnp.sum(probs, axis=-1, keepdims=True)
            mixed = mixed + jnp.dot(
                probs.astype(jnp.bfloat16), v_ref[:, lanes], preferred_element_type=jnp.float32
            )
        results.append(mixed / total)
    o_ref[...] = jnp.concatenate(results, axis=1).astype(o_ref.dtype)


def attention(image_qkv, keys_a, keys_b, valid):
    rows = image_qkv.shape[0]
    pairs = HEADS // 2
    width = 2 * HEAD_DIM

    def spec(array, offset):
        return pl.BlockSpec((array.shape[0], width), lambda j: (0, j + offset))

    return pl.pallas_call(
        attention_kernel,
        grid=(pairs,),
        in_specs=[
            spec(image_qkv, 0),
            spec(keys_a, 0),
            spec(keys_a, pairs),
            spec(keys_b, 0),
            spec(keys_b, pairs),
            pl.BlockSpec(valid.shape, lambda j: (0, 0)),
        ],
        out_specs=pl.BlockSpec((rows, width), lambda j: (0, j)),
        out_shape=jax.ShapeDtypeStruct((rows, HEADS * HEAD_DIM), jnp.bfloat16),
    )(image_qkv, keys_a, keys_a, keys_b, keys_b, valid)


def per_device(
    image_tokens,
    text_tokens,
    mod_image,
    mod_text,
    text_lengths,
    item_group,
    item_step,
    step_sizes,
    guide_scales,
    qkv_weight,
    kv_weight,
    out_weight,
):
    image_rows = image_tokens.shape[1]
    text_rows = text_tokens.shape[2]
    model_width = image_tokens.shape[2]
    heads_width = HEADS * HEAD_DIM
    picture = image_tokens[0]
    mod_one = mod_image[0, 0]
    mod_two = mod_text[0, 0]

    rep_size = lax.axis_size("rep")
    seq_size = lax.axis_size("seq")
    qkv_cols = qkv_weight.shape[1]
    kv_cols = kv_weight.shape[1]
    piece_rows = qkv_weight.shape[0]
    packed = jnp.concatenate(
        [qkv_weight, kv_weight, out_weight.reshape(piece_rows, -1)], axis=1
    )
    packed = ring_gather(packed, "rep", rep_size, 1, forward=False)
    packed = ring_gather(packed, "seq", *SEQ_X, forward=False)
    packed = packed.reshape(-1, packed.shape[-1])
    packed = ring_gather(packed, "seq", *SEQ_Z)
    packed = ring_gather(packed, "seq", *SEQ_Y)
    packed = packed.reshape(-1, packed.shape[-1])
    qkv_half = packed[:, :qkv_cols]
    kv_half = packed[:, qkv_cols : qkv_cols + kv_cols]
    out_half = packed[:, qkv_cols + kv_cols :].reshape(-1, out_weight.shape[1])
    cfg_index = lax.axis_index("cfg")
    source = (
        (
            slot_digits("seq", *SEQ_Y)[:, None, None, None] * SEQ_Y[1]
            + slot_digits("seq", *SEQ_Z)[None, :, None, None] * SEQ_Z[1]
            + slot_digits("seq", *SEQ_X)[None, None, :, None] * SEQ_X[1]
        )
        * rep_size
        + slot_digits("rep", rep_size, 1)[None, None, None, :]
    ).reshape(-1)

    def columns(half, rows):
        owner = half * (seq_size * rep_size) + source
        return (owner[:, None] * rows + jnp.arange(rows, dtype=jnp.int32)[None, :]).reshape(-1)

    own_text = text_tokens[0, 0].astype(jnp.float32)
    swapped = partner_2(jnp.concatenate([mod_one, own_text, mod_two]), "cfg", 0)
    mod_other = swapped[: mod_one.shape[0]]
    text_other = swapped[mod_one.shape[0] : mod_one.shape[0] + own_text.shape[0]]
    mod_text_other = swapped[mod_one.shape[0] + own_text.shape[0] :]

    def modulate(values, mod):
        return (layer_norm(values.astype(jnp.float32)) * (1.0 + mod[1]) + mod[0]).astype(
            jnp.bfloat16
        )

    image_mod = modulate(picture, mod_one)
    text_mod = modulate(text_tokens[0, 0], mod_two)
    image_other = modulate(picture, mod_other)
    text_other_mod = modulate(text_other, mod_text_other)
    feature_cols = columns(cfg_index, qkv_weight.shape[0])

    def project(values, weight):
        return jnp.dot(
            jnp.take(values, feature_cols, axis=1), weight, preferred_element_type=jnp.float32
        )

    sent = partner_2((project(image_other, qkv_half), project(text_other_mod, kv_half)), "cfg", 0)
    qkv_total = project(image_mod, qkv_half) + sent[0]
    kv_total = project(text_mod, kv_half) + sent[1]
    out_other = partner_2(out_half, "cfg", 0)
    image_qkv = qkv_total.astype(jnp.bfloat16)
    text_kv = kv_total.astype(jnp.bfloat16)
    length = text_lengths[0, 0]
    image_kv = image_qkv[:, heads_width:]

    cut = 64
    filler = (-(cut + text_rows)) % 16
    part_a = jnp.concatenate(
        [image_kv[:cut], text_kv, jnp.zeros((filler, image_kv.shape[1]), image_kv.dtype)]
    )
    part_a = ring_gather(part_a, "seq", *SEQ_Z)
    part_a = ring_gather(part_a, "seq", *SEQ_X)
    part_a = ring_gather(part_a, "seq", *SEQ_Y)
    part_b = ring_gather(image_kv[cut:], "seq", *SEQ_Z)
    part_b = ring_gather(part_b, "seq", *SEQ_Y)
    part_b = ring_gather(part_b, "seq", *SEQ_X)
    owner_a = (
        slot_digits("seq", *SEQ_Y)[:, None, None] * SEQ_Y[1]
        + slot_digits("seq", *SEQ_X)[None, :, None] * SEQ_X[1]
        + slot_digits("seq", *SEQ_Z)[None, None, :] * SEQ_Z[1]
    ).reshape(-1)
    row = jnp.arange(cut + text_rows + filler, dtype=jnp.int32)[None, :]
    position = owner_a[:, None] * text_rows + row - cut
    valid = (row < cut) | ((row < cut + text_rows) & (position < length))
    width = image_kv.shape[1]
    attended = attention(
        image_qkv,
        part_a.reshape(-1, width),
        part_b.reshape(-1, width),
        valid.astype(jnp.float32).reshape(1, -1),
    )
    out_rows = out_weight.shape[0]
    projected = jnp.dot(
        jnp.take(attended, columns(cfg_index, out_rows), axis=1),
        out_half,
        preferred_element_type=jnp.float32,
    ) + jnp.dot(
        jnp.take(attended, columns(1 - cfg_index, out_rows), axis=1),
        out_other,
        preferred_element_type=jnp.float32,
    )
    velocity = mod_one[2] * projected
    half_width = model_width // 2
    guide_scale = jnp.sum(
        jnp.where(
            jnp.arange(guide_scales.shape[0], dtype=jnp.int32) == item_group[0], guide_scales, 0.0
        )
    )
    step_size = jnp.sum(
        jnp.where(jnp.arange(step_sizes.shape[0], dtype=jnp.int32) == item_step[0], step_sizes, 0.0)
    )
    partner = partner_2(velocity.astype(jnp.bfloat16), "cfg", 0).astype(velocity.dtype)
    cond_full = jnp.where(cfg_index == 0, velocity, partner)
    uncond_full = jnp.where(cfg_index == 0, partner, velocity)
    conditional = lax.dynamic_slice_in_dim(cond_full, cfg_index * half_width, half_width, 1)
    unconditional = lax.dynamic_slice_in_dim(uncond_full, cfg_index * half_width, half_width, 1)
    guided = unconditional + guide_scale * (conditional - unconditional)
    base_part = lax.dynamic_slice_in_dim(picture, cfg_index * half_width, half_width, 1)
    return (base_part + step_size * guided)[None]


def solution(mesh):
    placed = (
        P("rep", "seq", None),
        P("cfg", "rep", "seq", None),
        P("cfg", "rep", None, None),
        P("cfg", "rep", None, None),
        P("cfg", "rep"),
        P("rep"),
        P("rep"),
        P(),
        P(),
        P(("cfg", "seq", "rep"), None),
        P(("cfg", "seq", "rep"), None),
        P(("cfg", "seq", "rep"), None),
    )
    return jax.shard_map(
        per_device, mesh=mesh, in_specs=placed, out_specs=P("rep", "seq", "cfg"), check_vma=False
    )
```

```python
import jax
import jax.numpy as jnp
from jax import lax
from jax.sharding import PartitionSpec as P
from jax.experimental import pallas as pl

HEADS = 12
HEAD_DIM = 64


def partner_2(x, axis, apart):
    return lax.ppermute(x, axis, [(i, i ^ 1 << apart) for i in range(lax.axis_size(axis))])


def digit_shift(count, size, stride, step):
    return [
        (i, i + ((i // stride + step) % size - (i // stride) % size) * stride) for i in range(count)
    ]


def ring_gather(x, axis, size, stride, forward=True):
    count = lax.axis_size(axis)
    tmap = jax.tree.map

    def send(v, step):
        return lax.ppermute(v, axis, digit_shift(count, size, stride, step))

    if size == 1:
        return tmap(lambda v: v[None], x)
    if size == 2:
        return tmap(lambda v, w: jnp.stack([v, w]), x, send(x, 1))
    assert size == 4
    from_left = send(x, 1)
    from_right = send(x, -1)
    if forward:
        head = send(tmap(lambda v: v[: v.shape[0] // 2], from_left), 1)
        tail = send(tmap(lambda v: v[v.shape[0] // 2 :], from_right), -1)
        far = tmap(lambda u, v: jnp.concatenate([u, v]), head, tail)
    else:
        far = send(x, 2)
    return tmap(lambda *vs: jnp.stack(vs), x, from_right, far, from_left)


def slot_digits(axis, size, stride):
    own = (lax.axis_index(axis) // stride) % size
    return (own + jnp.arange(size, dtype=jnp.int32)) % size


def staged_gather(parts, routes):
    for step in range(len(routes[0])):
        parts = tuple(
            ring_gather(part, *route[step]) if route[step] else part.reshape(-1, part.shape[-1])
            for part, route in zip(parts, routes)
        )
        parts = lax.optimization_barrier(parts)
    return parts


def route_owner(route, scale):
    owner = jnp.zeros((1,), jnp.int32)
    for stage in route:
        if stage:
            axis, size, stride = stage[:3]
            digits = slot_digits(axis, size, stride) * scale(axis, stride)
            owner = (digits[:, None] + owner[None, :]).reshape(-1)
    return owner


SEQ_X = (4, 1)
SEQ_Z = (2, 4)
SEQ_Y = (4, 8)


def layer_norm(values):
    row_mean = jnp.mean(values, axis=-1, keepdims=True)
    centred = values - row_mean
    row_var = jnp.mean(centred * centred, axis=-1, keepdims=True)
    return centred / jnp.sqrt(row_var + 1e-06)


def attention_kernel(q_ref, ka_ref, va_ref, kb_ref, vb_ref, valid_ref, o_ref):
    usable = valid_ref[...] > 0.0
    contract = (((1,), (1,)), ((), ()))
    results = []
    for head in range(2):
        lanes = slice(head * HEAD_DIM, (head + 1) * HEAD_DIM)
        query = q_ref[:, lanes]

        def scores(k_ref):
            return (
                lax.dot_general(query, k_ref[:, lanes], contract, preferred_element_type=jnp.float32)
                * 0.125
            )

        s_a = jnp.where(usable, scores(ka_ref), -1e30)
        s_b = scores(kb_ref)
        top = jnp.maximum(jnp.max(s_a, axis=-1, keepdims=True), jnp.max(s_b, axis=-1, keepdims=True))
        total = jnp.zeros((query.shape[0], 1), jnp.float32)
        mixed = jnp.zeros((query.shape[0], HEAD_DIM), jnp.float32)
        for part, v_ref in ((s_a, va_ref), (s_b, vb_ref)):
            probs = jnp.exp(part - top)
            total = total + jnp.sum(probs, axis=-1, keepdims=True)
            mixed = mixed + jnp.dot(
                probs.astype(jnp.bfloat16), v_ref[:, lanes], preferred_element_type=jnp.float32
            )
        results.append(mixed / total)
    o_ref[...] = jnp.concatenate(results, axis=1).astype(o_ref.dtype)


def attention(image_qkv, keys_a, keys_b, valid):
    rows = image_qkv.shape[0]
    pairs = HEADS // 2
    width = 2 * HEAD_DIM

    def spec(array, offset):
        return pl.BlockSpec((array.shape[0], width), lambda j: (0, j + offset))

    return pl.pallas_call(
        attention_kernel,
        grid=(pairs,),
        in_specs=[
            spec(image_qkv, 0),
            spec(keys_a, 0),
            spec(keys_a, pairs),
            spec(keys_b, 0),
            spec(keys_b, pairs),
            pl.BlockSpec(valid.shape, lambda j: (0, 0)),
        ],
        out_specs=pl.BlockSpec((rows, width), lambda j: (0, j)),
        out_shape=jax.ShapeDtypeStruct((rows, HEADS * HEAD_DIM), jnp.bfloat16),
    )(image_qkv, keys_a, keys_a, keys_b, keys_b, valid)


def per_device(
    image_tokens,
    text_tokens,
    mod_image,
    mod_text,
    text_lengths,
    item_group,
    item_step,
    step_sizes,
    guide_scales,
    qkv_weight,
    kv_weight,
    out_weight,
):
    image_rows = image_tokens.shape[1]
    text_rows = text_tokens.shape[2]
    model_width = image_tokens.shape[2]
    heads_width = HEADS * HEAD_DIM
    picture = image_tokens[0]
    mod_one = mod_image[0, 0]
    mod_two = mod_text[0, 0]

    rep_size = lax.axis_size("rep")
    seq_size = lax.axis_size("seq")
    piece_rows = qkv_weight.shape[0]
    rep_route = ("rep", rep_size, 1, False)
    z_route = ("seq", *SEQ_Z)
    route_a = (rep_route, z_route, None, ("seq", *SEQ_X), ("seq", *SEQ_Y))
    route_b = (rep_route, z_route, None, ("seq", *SEQ_Y), ("seq", *SEQ_X))
    qkv_half, rest_half = staged_gather(
        (qkv_weight, jnp.concatenate([kv_weight, out_weight.reshape(piece_rows, -1)], axis=1)),
        (route_a, route_b),
    )
    qkv_half = qkv_half.reshape(-1, qkv_half.shape[-1])
    rest_half = rest_half.reshape(-1, rest_half.shape[-1])
    kv_cols = kv_weight.shape[1]
    kv_half = rest_half[:, :kv_cols]
    out_half = rest_half[:, kv_cols:].reshape(-1, out_weight.shape[1])
    cfg_index = lax.axis_index("cfg")

    def weight_scale(axis, stride):
        return stride * rep_size if axis == "seq" else stride

    source_a = route_owner(route_a, weight_scale)
    source_b = route_owner(route_b, weight_scale)

    def columns(half, rows, source):
        owner = half * (seq_size * rep_size) + source
        return (owner[:, None] * rows + jnp.arange(rows, dtype=jnp.int32)[None, :]).reshape(-1)

    own_text = text_tokens[0, 0].astype(jnp.float32)
    swapped = partner_2(jnp.concatenate([mod_one, own_text, mod_two]), "cfg", 0)
    mod_other = swapped[: mod_one.shape[0]]
    text_other = swapped[mod_one.shape[0] : mod_one.shape[0] + own_text.shape[0]]
    mod_text_other = swapped[mod_one.shape[0] + own_text.shape[0] :]

    def modulate(values, mod):
        return (layer_norm(values.astype(jnp.float32)) * (1.0 + mod[1]) + mod[0]).astype(
            jnp.bfloat16
        )

    image_mod = modulate(picture, mod_one)
    text_mod = modulate(text_tokens[0, 0], mod_two)
    image_other = modulate(picture, mod_other)
    text_other_mod = modulate(text_other, mod_text_other)
    cols_a = columns(cfg_index, piece_rows, source_a)
    cols_b = columns(cfg_index, piece_rows, source_b)

    def project(values, weight, cols):
        return jnp.dot(jnp.take(values, cols, axis=1), weight, preferred_element_type=jnp.float32)

    sent = partner_2(
        (project(image_other, qkv_half, cols_a), project(text_other_mod, kv_half, cols_b)), "cfg", 0
    )
    qkv_total = project(image_mod, qkv_half, cols_a) + sent[0]
    kv_total = project(text_mod, kv_half, cols_b) + sent[1]
    out_other = partner_2(out_half, "cfg", 0)
    image_qkv = qkv_total.astype(jnp.bfloat16)
    text_kv = kv_total.astype(jnp.bfloat16)
    length = text_lengths[0, 0]
    image_kv = image_qkv[:, heads_width:]

    cut = 64
    filler = (-(cut + text_rows)) % 16
    part_a = jnp.concatenate(
        [image_kv[:cut], text_kv, jnp.zeros((filler, image_kv.shape[1]), image_kv.dtype)]
    )
    kv_route_a = (("seq", *SEQ_Z), ("seq", *SEQ_X), ("seq", *SEQ_Y))
    kv_route_b = (("seq", *SEQ_Z), ("seq", *SEQ_Y), ("seq", *SEQ_X))
    part_a, part_b = staged_gather((part_a, image_kv[cut:]), (kv_route_a, kv_route_b))
    owner_a = route_owner(kv_route_a, lambda axis, stride: stride)
    row = jnp.arange(cut + text_rows + filler, dtype=jnp.int32)[None, :]
    position = owner_a[:, None] * text_rows + row - cut
    valid = (row < cut) | ((row < cut + text_rows) & (position < length))
    width = image_kv.shape[1]
    attended = attention(
        image_qkv,
        part_a.reshape(-1, width),
        part_b.reshape(-1, width),
        valid.astype(jnp.float32).reshape(1, -1),
    )
    out_rows = out_weight.shape[0]
    projected = jnp.dot(
        jnp.take(attended, columns(cfg_index, out_rows, source_b), axis=1),
        out_half,
        preferred_element_type=jnp.float32,
    ) + jnp.dot(
        jnp.take(attended, columns(1 - cfg_index, out_rows, source_b), axis=1),
        out_other,
        preferred_element_type=jnp.float32,
    )
    velocity = mod_one[2] * projected
    half_width = model_width // 2
    guide_scale = jnp.sum(
        jnp.where(
            jnp.arange(guide_scales.shape[0], dtype=jnp.int32) == item_group[0], guide_scales, 0.0
        )
    )
    step_size = jnp.sum(
        jnp.where(jnp.arange(step_sizes.shape[0], dtype=jnp.int32) == item_step[0], step_sizes, 0.0)
    )
    partner = partner_2(velocity.astype(jnp.bfloat16), "cfg", 0).astype(velocity.dtype)
    cond_full = jnp.where(cfg_index == 0, velocity, partner)
    uncond_full = jnp.where(cfg_index == 0, partner, velocity)
    conditional = lax.dynamic_slice_in_dim(cond_full, cfg_index * half_width, half_width, 1)
    unconditional = lax.dynamic_slice_in_dim(uncond_full, cfg_index * half_width, half_width, 1)
    guided = unconditional + guide_scale * (conditional - unconditional)
    base_part = lax.dynamic_slice_in_dim(picture, cfg_index * half_width, half_width, 1)
    return (base_part + step_size * guided)[None]


def solution(mesh):
    placed = (
        P("rep", "seq", None),
        P("cfg", "rep", "seq", None),
        P("cfg", "rep", None, None),
        P("cfg", "rep", None, None),
        P("cfg", "rep"),
        P("rep"),
        P("rep"),
        P(),
        P(),
        P(("cfg", "seq", "rep"), None),
        P(("cfg", "seq", "rep"), None),
        P(("cfg", "seq", "rep"), None),
    )
    return jax.shard_map(
        per_device, mesh=mesh, in_specs=placed, out_specs=P("rep", "seq", "cfg"), check_vma=False
    )
```

```python
import jax
import jax.numpy as jnp
from jax import lax
from jax.sharding import PartitionSpec as P
from jax.experimental import pallas as pl

HEADS = 12
HEAD_DIM = 64


def partner_2(x, axis, apart):
    return lax.ppermute(x, axis, [(i, i ^ 1 << apart) for i in range(lax.axis_size(axis))])


def digit_shift(count, size, stride, step):
    return [
        (i, i + ((i // stride + step) % size - (i // stride) % size) * stride) for i in range(count)
    ]


def ring_gather(x, axis, size, stride, forward=True):
    count = lax.axis_size(axis)
    tmap = jax.tree.map

    def send(v, step):
        return lax.ppermute(v, axis, digit_shift(count, size, stride, step))

    if size == 1:
        return tmap(lambda v: v[None], x)
    if size == 2:
        return tmap(lambda v, w: jnp.stack([v, w]), x, send(x, 1))
    assert size == 4
    from_left = send(x, 1)
    from_right = send(x, -1)
    if forward:
        head = send(tmap(lambda v: v[: v.shape[0] // 2], from_left), 1)
        tail = send(tmap(lambda v: v[v.shape[0] // 2 :], from_right), -1)
        far = tmap(lambda u, v: jnp.concatenate([u, v]), head, tail)
    else:
        far = send(x, 2)
    return tmap(lambda *vs: jnp.stack(vs), x, from_right, far, from_left)


def slot_digits(axis, size, stride):
    own = (lax.axis_index(axis) // stride) % size
    return (own + jnp.arange(size, dtype=jnp.int32)) % size


def staged_gather(parts, routes):
    for step in range(len(routes[0])):
        parts = tuple(
            ring_gather(part, *route[step]) if route[step] else part.reshape(-1, part.shape[-1])
            for part, route in zip(parts, routes)
        )
        parts = lax.optimization_barrier(parts)
    return parts


def route_owner(route, scale):
    owner = jnp.zeros((1,), jnp.int32)
    for stage in route:
        if stage:
            axis, size, stride = stage[:3]
            digits = slot_digits(axis, size, stride) * scale(axis, stride)
            owner = (digits[:, None] + owner[None, :]).reshape(-1)
    return owner


SEQ_X = (4, 1)
SEQ_Z = (2, 4)
SEQ_Y = (4, 8)


def layer_norm(values):
    row_mean = jnp.mean(values, axis=-1, keepdims=True)
    centred = values - row_mean
    row_var = jnp.mean(centred * centred, axis=-1, keepdims=True)
    return centred / jnp.sqrt(row_var + 1e-06)


def attention_kernel(q_ref, ka_ref, va_ref, kb_ref, vb_ref, valid_ref, o_ref):
    usable = valid_ref[...] > 0.0
    contract = (((1,), (1,)), ((), ()))
    results = []
    for head in range(2):
        lanes = slice(head * HEAD_DIM, (head + 1) * HEAD_DIM)
        query = q_ref[:, lanes]

        def scores(k_ref):
            return (
                lax.dot_general(query, k_ref[:, lanes], contract, preferred_element_type=jnp.float32)
                * 0.125
            )

        s_a = jnp.where(usable, scores(ka_ref), -1e30)
        s_b = scores(kb_ref)
        top = jnp.maximum(jnp.max(s_a, axis=-1, keepdims=True), jnp.max(s_b, axis=-1, keepdims=True))
        total = jnp.zeros((query.shape[0], 1), jnp.float32)
        mixed = jnp.zeros((query.shape[0], HEAD_DIM), jnp.float32)
        for part, v_ref in ((s_a, va_ref), (s_b, vb_ref)):
            probs = jnp.exp(part - top)
            total = total + jnp.sum(probs, axis=-1, keepdims=True)
            mixed = mixed + jnp.dot(
                probs.astype(jnp.bfloat16), v_ref[:, lanes], preferred_element_type=jnp.float32
            )
        results.append(mixed / total)
    o_ref[...] = jnp.concatenate(results, axis=1).astype(o_ref.dtype)


def attention(image_qkv, keys_a, keys_b, valid):
    rows = image_qkv.shape[0]
    pairs = HEADS // 2
    width = 2 * HEAD_DIM

    def spec(array, offset):
        return pl.BlockSpec((array.shape[0], width), lambda j: (0, j + offset))

    return pl.pallas_call(
        attention_kernel,
        grid=(pairs,),
        in_specs=[
            spec(image_qkv, 0),
            spec(keys_a, 0),
            spec(keys_a, pairs),
            spec(keys_b, 0),
            spec(keys_b, pairs),
            pl.BlockSpec(valid.shape, lambda j: (0, 0)),
        ],
        out_specs=pl.BlockSpec((rows, width), lambda j: (0, j)),
        out_shape=jax.ShapeDtypeStruct((rows, HEADS * HEAD_DIM), jnp.bfloat16),
    )(image_qkv, keys_a, keys_a, keys_b, keys_b, valid)


def reorder(values, cols):
    picks = jnp.arange(values.shape[1], dtype=jnp.int32)[:, None] == cols[None, :]
    return jnp.dot(values, picks.astype(values.dtype), preferred_element_type=jnp.float32).astype(
        values.dtype
    )


def per_device(
    image_tokens,
    text_tokens,
    mod_image,
    mod_text,
    text_lengths,
    item_group,
    item_step,
    step_sizes,
    guide_scales,
    qkv_weight,
    kv_weight,
    out_weight,
):
    image_rows = image_tokens.shape[1]
    text_rows = text_tokens.shape[2]
    model_width = image_tokens.shape[2]
    heads_width = HEADS * HEAD_DIM
    picture = image_tokens[0]
    mod_one = mod_image[0, 0]
    mod_two = mod_text[0, 0]

    rep_size = lax.axis_size("rep")
    seq_size = lax.axis_size("seq")
    piece_rows = qkv_weight.shape[0]
    rep_route = ("rep", rep_size, 1, False)
    z_route = ("seq", *SEQ_Z)
    route_a = (rep_route, z_route, None, ("seq", *SEQ_X), ("seq", *SEQ_Y))
    route_b = (rep_route, z_route, None, ("seq", *SEQ_Y), ("seq", *SEQ_X))
    qkv_cols = qkv_weight.shape[1]
    (packed,) = staged_gather(
        (jnp.concatenate([qkv_weight, kv_weight, out_weight.reshape(piece_rows, -1)], axis=1),),
        (route_a[:3],),
    )
    qkv_half, rest_half = staged_gather(
        (packed[:, :qkv_cols], packed[:, qkv_cols:]), (route_a[3:], route_b[3:])
    )
    qkv_half = qkv_half.reshape(-1, qkv_half.shape[-1])
    rest_half = rest_half.reshape(-1, rest_half.shape[-1])
    kv_cols = kv_weight.shape[1]
    kv_half = rest_half[:, :kv_cols]
    out_half = rest_half[:, kv_cols:].reshape(-1, out_weight.shape[1])
    cfg_index = lax.axis_index("cfg")

    def weight_scale(axis, stride):
        return stride * rep_size if axis == "seq" else stride

    source_a = route_owner(route_a, weight_scale)
    source_b = route_owner(route_b, weight_scale)

    def columns(half, rows, source):
        owner = half * (seq_size * rep_size) + source
        return (owner[:, None] * rows + jnp.arange(rows, dtype=jnp.int32)[None, :]).reshape(-1)

    own_text = text_tokens[0, 0].astype(jnp.float32)
    swapped = partner_2(jnp.concatenate([mod_one, own_text, mod_two]), "cfg", 0)
    mod_other = swapped[: mod_one.shape[0]]
    text_other = swapped[mod_one.shape[0] : mod_one.shape[0] + own_text.shape[0]]
    mod_text_other = swapped[mod_one.shape[0] + own_text.shape[0] :]

    def modulate(values, mod):
        return (layer_norm(values.astype(jnp.float32)) * (1.0 + mod[1]) + mod[0]).astype(
            jnp.bfloat16
        )

    image_mod = modulate(picture, mod_one)
    text_mod = modulate(text_tokens[0, 0], mod_two)
    image_other = modulate(picture, mod_other)
    text_other_mod = modulate(text_other, mod_text_other)
    cols_a = columns(cfg_index, piece_rows, source_a)
    cols_b = columns(cfg_index, piece_rows, source_b)

    def project(values, weight, cols):
        return jnp.dot(reorder(values, cols), weight, preferred_element_type=jnp.float32)

    sent = partner_2(
        (project(image_other, qkv_half, cols_a), project(text_other_mod, kv_half, cols_b)), "cfg", 0
    )
    qkv_total = project(image_mod, qkv_half, cols_a) + sent[0]
    kv_total = project(text_mod, kv_half, cols_b) + sent[1]
    out_other = partner_2(out_half, "cfg", 0)
    image_qkv = qkv_total.astype(jnp.bfloat16)
    text_kv = kv_total.astype(jnp.bfloat16)
    length = text_lengths[0, 0]
    image_kv = image_qkv[:, heads_width:]

    cut = 64
    filler = (-(cut + text_rows)) % 16
    local = jnp.concatenate(
        [image_kv[:cut], text_kv, jnp.zeros((filler, image_kv.shape[1]), image_kv.dtype), image_kv[cut:]]
    )
    kv_route_a = (("seq", *SEQ_Z), ("seq", *SEQ_X), ("seq", *SEQ_Y))
    kv_route_b = (("seq", *SEQ_Z), ("seq", *SEQ_Y), ("seq", *SEQ_X))
    (local,) = staged_gather((local,), (kv_route_a[:1],))
    split = cut + text_rows + filler
    part_a, part_b = staged_gather(
        (local[:, :split], local[:, split:]), (kv_route_a[1:], kv_route_b[1:])
    )
    owner_a = route_owner(kv_route_a, lambda axis, stride: stride)
    row = jnp.arange(cut + text_rows + filler, dtype=jnp.int32)[None, :]
    position = owner_a[:, None] * text_rows + row - cut
    valid = (row < cut) | ((row < cut + text_rows) & (position < length))
    width = image_kv.shape[1]
    attended = attention(
        image_qkv,
        part_a.reshape(-1, width),
        part_b.reshape(-1, width),
        valid.astype(jnp.float32).reshape(1, -1),
    )
    out_rows = out_weight.shape[0]
    projected = jnp.dot(
        reorder(attended, columns(cfg_index, out_rows, source_b)),
        out_half,
        preferred_element_type=jnp.float32,
    ) + jnp.dot(
        reorder(attended, columns(1 - cfg_index, out_rows, source_b)),
        out_other,
        preferred_element_type=jnp.float32,
    )
    velocity = mod_one[2] * projected
    half_width = model_width // 2
    guide_scale = jnp.sum(
        jnp.where(
            jnp.arange(guide_scales.shape[0], dtype=jnp.int32) == item_group[0], guide_scales, 0.0
        )
    )
    step_size = jnp.sum(
        jnp.where(jnp.arange(step_sizes.shape[0], dtype=jnp.int32) == item_step[0], step_sizes, 0.0)
    )
    partner = partner_2(velocity.astype(jnp.bfloat16), "cfg", 0).astype(velocity.dtype)
    cond_full = jnp.where(cfg_index == 0, velocity, partner)
    uncond_full = jnp.where(cfg_index == 0, partner, velocity)
    conditional = lax.dynamic_slice_in_dim(cond_full, cfg_index * half_width, half_width, 1)
    unconditional = lax.dynamic_slice_in_dim(uncond_full, cfg_index * half_width, half_width, 1)
    guided = unconditional + guide_scale * (conditional - unconditional)
    base_part = lax.dynamic_slice_in_dim(picture, cfg_index * half_width, half_width, 1)
    return (base_part + step_size * guided)[None]


def solution(mesh):
    placed = (
        P("rep", "seq", None),
        P("cfg", "rep", "seq", None),
        P("cfg", "rep", None, None),
        P("cfg", "rep", None, None),
        P("cfg", "rep"),
        P("rep"),
        P("rep"),
        P(),
        P(),
        P(("cfg", "seq", "rep"), None),
        P(("cfg", "seq", "rep"), None),
        P(("cfg", "seq", "rep"), None),
    )
    return jax.shard_map(
        per_device, mesh=mesh, in_specs=placed, out_specs=P("rep", "seq", "cfg"), check_vma=False
    )
```

```python
import functools

import jax
import jax.numpy as jnp
from jax import lax
from jax.sharding import PartitionSpec as P
from jax.experimental import pallas as pl

HEADS = 12
HEAD_DIM = 64


def partner_2(x, axis, apart):
    return lax.ppermute(x, axis, [(i, i ^ 1 << apart) for i in range(lax.axis_size(axis))])


def digit_shift(count, size, stride, step):
    return [
        (i, i + ((i // stride + step) % size - (i // stride) % size) * stride) for i in range(count)
    ]


def ring_gather(x, axis, size, stride, forward=True):
    count = lax.axis_size(axis)
    tmap = jax.tree.map

    def send(v, step):
        return lax.ppermute(v, axis, digit_shift(count, size, stride, step))

    if size == 1:
        return tmap(lambda v: v[None], x)
    if size == 2:
        return tmap(lambda v, w: jnp.stack([v, w]), x, send(x, 1))
    assert size == 4
    from_left = send(x, 1)
    from_right = send(x, -1)
    if forward:
        head = send(tmap(lambda v: v[: v.shape[0] // 2], from_left), 1)
        tail = send(tmap(lambda v: v[v.shape[0] // 2 :], from_right), -1)
        far = tmap(lambda u, v: jnp.concatenate([u, v]), head, tail)
    else:
        far = send(x, 2)
    return tmap(lambda *vs: jnp.stack(vs), x, from_right, far, from_left)


def ring_pieces(x, axis, size, stride):
    count = lax.axis_size(axis)

    def send(v, step):
        return lax.ppermute(v, axis, digit_shift(count, size, stride, step))

    assert size == 4
    from_left = send(x, 1)
    from_right = send(x, -1)
    half = x.shape[0] // 2
    return [x, from_right, send(from_left[:half], 1), send(from_right[half:], -1), from_left]


def piece_owners(prev, digits):
    half = prev.shape[0] // 2
    return [
        digits[0] + prev,
        digits[1] + prev,
        digits[2] + prev[:half],
        digits[2] + prev[half:],
        digits[3] + prev,
    ]


def slot_digits(axis, size, stride):
    own = (lax.axis_index(axis) // stride) % size
    return (own + jnp.arange(size, dtype=jnp.int32)) % size


def staged_gather(parts, routes):
    for step in range(len(routes[0])):
        parts = tuple(
            ring_gather(part, *route[step]) if route[step] else part.reshape(-1, part.shape[-1])
            for part, route in zip(parts, routes)
        )
        parts = lax.optimization_barrier(parts)
    return parts


def route_owner(route, scale):
    owner = jnp.zeros((1,), jnp.int32)
    for stage in route:
        if stage:
            axis, size, stride = stage[:3]
            digits = slot_digits(axis, size, stride) * scale(axis, stride)
            owner = (digits[:, None] + owner[None, :]).reshape(-1)
    return owner


SEQ_X = (4, 1)
SEQ_Z = (2, 4)
SEQ_Y = (4, 8)


def layer_norm(values):
    row_mean = jnp.mean(values, axis=-1, keepdims=True)
    centred = values - row_mean
    row_var = jnp.mean(centred * centred, axis=-1, keepdims=True)
    return centred / jnp.sqrt(row_var + 1e-06)


def attention_kernel(*refs, masked):
    q_ref, o_ref = refs[0], refs[-1]
    count = len(masked)
    key_refs = refs[1 : 1 + 2 * count : 2]
    value_refs = refs[2 : 2 + 2 * count : 2]
    mask_refs = iter(refs[1 + 2 * count : -1])
    masks = [next(mask_refs)[...] > 0.0 if m else None for m in masked]
    contract = (((1,), (1,)), ((), ()))
    results = []
    for head in range(2):
        lanes = slice(head * HEAD_DIM, (head + 1) * HEAD_DIM)
        query = q_ref[:, lanes]
        parts = []
        for k_ref, usable in zip(key_refs, masks):
            part = (
                lax.dot_general(query, k_ref[:, lanes], contract, preferred_element_type=jnp.float32)
                * 0.125
            )
            parts.append(part if usable is None else jnp.where(usable, part, -1e30))
        top = jnp.max(parts[0], axis=-1, keepdims=True)
        for part in parts[1:]:
            top = jnp.maximum(top, jnp.max(part, axis=-1, keepdims=True))
        total = jnp.zeros((query.shape[0], 1), jnp.float32)
        mixed = jnp.zeros((query.shape[0], HEAD_DIM), jnp.float32)
        for part, v_ref in zip(parts, value_refs):
            probs = jnp.exp(part - top)
            total = total + jnp.sum(probs, axis=-1, keepdims=True)
            mixed = mixed + jnp.dot(
                probs.astype(jnp.bfloat16), v_ref[:, lanes], preferred_element_type=jnp.float32
            )
        results.append(mixed / total)
    o_ref[...] = jnp.concatenate(results, axis=1).astype(o_ref.dtype)


def attention(image_qkv, pieces, masks):
    rows = image_qkv.shape[0]
    pairs = HEADS // 2
    width = 2 * HEAD_DIM

    def spec(array, offset):
        return pl.BlockSpec((array.shape[0], width), lambda j: (0, j + offset))

    operands = [image_qkv]
    in_specs = [spec(image_qkv, 0)]
    for piece in pieces:
        operands += [piece, piece]
        in_specs += [spec(piece, 0), spec(piece, pairs)]
    for mask in masks:
        if mask is not None:
            operands.append(mask)
            in_specs.append(pl.BlockSpec(mask.shape, lambda j: (0, 0)))
    kernel = functools.partial(attention_kernel, masked=tuple(m is not None for m in masks))
    return pl.pallas_call(
        kernel,
        grid=(pairs,),
        in_specs=in_specs,
        out_specs=pl.BlockSpec((rows, width), lambda j: (0, j)),
        out_shape=jax.ShapeDtypeStruct((rows, HEADS * HEAD_DIM), jnp.bfloat16),
    )(*operands)


def reorder(values, cols):
    picks = jnp.arange(values.shape[1], dtype=jnp.int32)[:, None] == cols[None, :]
    return jnp.dot(values, picks.astype(values.dtype), preferred_element_type=jnp.float32).astype(
        values.dtype
    )


def per_device(
    image_tokens,
    text_tokens,
    mod_image,
    mod_text,
    text_lengths,
    item_group,
    item_step,
    step_sizes,
    guide_scales,
    qkv_weight,
    kv_weight,
    out_weight,
):
    image_rows = image_tokens.shape[1]
    text_rows = text_tokens.shape[2]
    model_width = image_tokens.shape[2]
    heads_width = HEADS * HEAD_DIM
    picture = image_tokens[0]
    mod_one = mod_image[0, 0]
    mod_two = mod_text[0, 0]

    rep_size = lax.axis_size("rep")
    seq_size = lax.axis_size("seq")
    piece_rows = qkv_weight.shape[0]
    rep_route = ("rep", rep_size, 1, False)
    z_route = ("seq", *SEQ_Z)
    route_a = (rep_route, z_route, None, ("seq", *SEQ_X), ("seq", *SEQ_Y))
    route_b = (rep_route, z_route, None, ("seq", *SEQ_Y), ("seq", *SEQ_X))
    qkv_cols = qkv_weight.shape[1]
    (packed,) = staged_gather(
        (jnp.concatenate([qkv_weight, kv_weight, out_weight.reshape(piece_rows, -1)], axis=1),),
        (route_a[:3],),
    )
    qkv_half, rest_half = staged_gather(
        (packed[:, :qkv_cols], packed[:, qkv_cols:]), (route_a[3:], route_b[3:])
    )
    qkv_half = qkv_half.reshape(-1, qkv_half.shape[-1])
    rest_half = rest_half.reshape(-1, rest_half.shape[-1])
    kv_cols = kv_weight.shape[1]
    kv_half = rest_half[:, :kv_cols]
    out_half = rest_half[:, kv_cols:].reshape(-1, out_weight.shape[1])
    cfg_index = lax.axis_index("cfg")

    def weight_scale(axis, stride):
        return stride * rep_size if axis == "seq" else stride

    source_a = route_owner(route_a, weight_scale)
    source_b = route_owner(route_b, weight_scale)

    def columns(half, rows, source):
        owner = half * (seq_size * rep_size) + source
        return (owner[:, None] * rows + jnp.arange(rows, dtype=jnp.int32)[None, :]).reshape(-1)

    own_text = text_tokens[0, 0].astype(jnp.float32)
    swapped = partner_2(jnp.concatenate([mod_one, own_text, mod_two]), "cfg", 0)
    mod_other = swapped[: mod_one.shape[0]]
    text_other = swapped[mod_one.shape[0] : mod_one.shape[0] + own_text.shape[0]]
    mod_text_other = swapped[mod_one.shape[0] + own_text.shape[0] :]

    def modulate(values, mod):
        return (layer_norm(values.astype(jnp.float32)) * (1.0 + mod[1]) + mod[0]).astype(
            jnp.bfloat16
        )

    image_mod = modulate(picture, mod_one)
    text_mod = modulate(text_tokens[0, 0], mod_two)
    image_other = modulate(picture, mod_other)
    text_other_mod = modulate(text_other, mod_text_other)
    cols_a = columns(cfg_index, piece_rows, source_a)
    cols_b = columns(cfg_index, piece_rows, source_b)

    def project(values, weight, cols):
        return jnp.dot(reorder(values, cols), weight, preferred_element_type=jnp.float32)

    sent = partner_2(
        (project(image_other, qkv_half, cols_a), project(text_other_mod, kv_half, cols_b)), "cfg", 0
    )
    qkv_total = project(image_mod, qkv_half, cols_a) + sent[0]
    kv_total = project(text_mod, kv_half, cols_b) + sent[1]
    out_other = partner_2(out_half, "cfg", 0)
    image_qkv = qkv_total.astype(jnp.bfloat16)
    text_kv = kv_total.astype(jnp.bfloat16)
    length = text_lengths[0, 0]
    image_kv = image_qkv[:, heads_width:]

    cut = 64
    filler = (-(cut + text_rows)) % 16
    local = jnp.concatenate(
        [image_kv[:cut], text_kv, jnp.zeros((filler, image_kv.shape[1]), image_kv.dtype), image_kv[cut:]]
    )
    kv_route_a = (("seq", *SEQ_Z), ("seq", *SEQ_X), ("seq", *SEQ_Y))
    kv_route_b = (("seq", *SEQ_Z), ("seq", *SEQ_Y), ("seq", *SEQ_X))
    (local,) = staged_gather((local,), (kv_route_a[:1],))
    split = cut + text_rows + filler
    part_a, part_b = staged_gather(
        (local[:, :split], local[:, split:]), (kv_route_a[1:2], kv_route_b[1:2])
    )
    pieces_a = ring_pieces(part_a, "seq", *SEQ_Y)
    pieces_b = ring_pieces(part_b, "seq", *SEQ_X)
    owners = piece_owners(
        route_owner(kv_route_a[:2], lambda axis, stride: stride),
        slot_digits("seq", *SEQ_Y) * SEQ_Y[1],
    )
    row = jnp.arange(split, dtype=jnp.int32)[None, :]
    width = image_kv.shape[1]
    masks = []
    for owner in owners:
        position = owner[:, None] * text_rows + row - cut
        valid = (row < cut) | ((row < cut + text_rows) & (position < length))
        masks.append(valid.astype(jnp.float32).reshape(1, -1))
    attended = attention(
        image_qkv,
        [p.reshape(-1, width) for p in pieces_a + pieces_b],
        masks + [None] * len(pieces_b),
    )
    out_rows = out_weight.shape[0]
    projected = jnp.dot(
        reorder(attended, columns(cfg_index, out_rows, source_b)),
        out_half,
        preferred_element_type=jnp.float32,
    ) + jnp.dot(
        reorder(attended, columns(1 - cfg_index, out_rows, source_b)),
        out_other,
        preferred_element_type=jnp.float32,
    )
    velocity = mod_one[2] * projected
    half_width = model_width // 2
    guide_scale = jnp.sum(
        jnp.where(
            jnp.arange(guide_scales.shape[0], dtype=jnp.int32) == item_group[0], guide_scales, 0.0
        )
    )
    step_size = jnp.sum(
        jnp.where(jnp.arange(step_sizes.shape[0], dtype=jnp.int32) == item_step[0], step_sizes, 0.0)
    )
    partner = partner_2(velocity.astype(jnp.bfloat16), "cfg", 0).astype(velocity.dtype)
    cond_full = jnp.where(cfg_index == 0, velocity, partner)
    uncond_full = jnp.where(cfg_index == 0, partner, velocity)
    conditional = lax.dynamic_slice_in_dim(cond_full, cfg_index * half_width, half_width, 1)
    unconditional = lax.dynamic_slice_in_dim(uncond_full, cfg_index * half_width, half_width, 1)
    guided = unconditional + guide_scale * (conditional - unconditional)
    base_part = lax.dynamic_slice_in_dim(picture, cfg_index * half_width, half_width, 1)
    return (base_part + step_size * guided)[None]


def solution(mesh):
    placed = (
        P("rep", "seq", None),
        P("cfg", "rep", "seq", None),
        P("cfg", "rep", None, None),
        P("cfg", "rep", None, None),
        P("cfg", "rep"),
        P("rep"),
        P("rep"),
        P(),
        P(),
        P(("cfg", "seq", "rep"), None),
        P(("cfg", "seq", "rep"), None),
        P(("cfg", "seq", "rep"), None),
    )
    return jax.shard_map(
        per_device, mesh=mesh, in_specs=placed, out_specs=P("rep", "seq", "cfg"), check_vma=False
    )
```

```python
import functools

import jax
import jax.numpy as jnp
from jax import lax
from jax.sharding import PartitionSpec as P
from jax.experimental import pallas as pl

HEADS = 12
HEAD_DIM = 64


def partner_2(x, axis, apart):
    return lax.ppermute(x, axis, [(i, i ^ 1 << apart) for i in range(lax.axis_size(axis))])


def digit_shift(count, size, stride, step):
    return [
        (i, i + ((i // stride + step) % size - (i // stride) % size) * stride) for i in range(count)
    ]


def ring_gather(x, axis, size, stride, forward=True):
    count = lax.axis_size(axis)
    tmap = jax.tree.map

    def send(v, step):
        return lax.ppermute(v, axis, digit_shift(count, size, stride, step))

    if size == 1:
        return tmap(lambda v: v[None], x)
    if size == 2:
        return tmap(lambda v, w: jnp.stack([v, w]), x, send(x, 1))
    assert size == 4
    from_left = send(x, 1)
    from_right = send(x, -1)
    if forward:
        head = send(tmap(lambda v: v[: v.shape[0] // 2], from_left), 1)
        tail = send(tmap(lambda v: v[v.shape[0] // 2 :], from_right), -1)
        far = tmap(lambda u, v: jnp.concatenate([u, v]), head, tail)
    else:
        far = send(x, 2)
    return tmap(lambda *vs: jnp.stack(vs), x, from_right, far, from_left)


def ring_pieces(x, axis, size, stride):
    count = lax.axis_size(axis)

    def send(v, step):
        return lax.ppermute(v, axis, digit_shift(count, size, stride, step))

    assert size == 4
    from_left = send(x, 1)
    from_right = send(x, -1)
    half = x.shape[0] // 2
    return [x, from_right, send(from_left[:half], 1), send(from_right[half:], -1), from_left]


def piece_owners(prev, digits):
    half = prev.shape[0] // 2
    return [
        digits[0] + prev,
        digits[1] + prev,
        digits[2] + prev[:half],
        digits[2] + prev[half:],
        digits[3] + prev,
    ]


def slot_digits(axis, size, stride):
    own = (lax.axis_index(axis) // stride) % size
    return (own + jnp.arange(size, dtype=jnp.int32)) % size


def staged_gather(parts, routes):
    for step in range(len(routes[0])):
        parts = tuple(
            ring_gather(part, *route[step]) if route[step] else part.reshape(-1, part.shape[-1])
            for part, route in zip(parts, routes)
        )
        parts = lax.optimization_barrier(parts)
    return parts


def route_owner(route, scale):
    owner = jnp.zeros((1,), jnp.int32)
    for stage in route:
        if stage:
            axis, size, stride = stage[:3]
            digits = slot_digits(axis, size, stride) * scale(axis, stride)
            owner = (digits[:, None] + owner[None, :]).reshape(-1)
    return owner


SEQ_X = (4, 1)
SEQ_Z = (2, 4)
SEQ_Y = (4, 8)


def layer_norm(values):
    row_mean = jnp.mean(values, axis=-1, keepdims=True)
    centred = values - row_mean
    row_var = jnp.mean(centred * centred, axis=-1, keepdims=True)
    return centred / jnp.sqrt(row_var + 1e-06)


def attention_kernel(*refs, masked, carry, final):
    count = len(masked)
    q_ref = refs[0]
    key_refs = refs[1 : 1 + 2 * count : 2]
    value_refs = refs[2 : 2 + 2 * count : 2]
    rest = list(refs[1 + 2 * count :])
    masks = [rest.pop(0)[...] > 0.0 if m else None for m in masked]
    if carry:
        top_in, total_in, mixed_in = rest[0][...], rest[1][...], rest[2][...]
        rest = rest[3:]
    contract = (((1,), (1,)), ((), ()))
    tops, totals, mixes = [], [], []
    for head in range(2):
        lanes = slice(head * HEAD_DIM, (head + 1) * HEAD_DIM)
        query = q_ref[:, lanes]
        parts = []
        for k_ref, usable in zip(key_refs, masks):
            part = (
                lax.dot_general(query, k_ref[:, lanes], contract, preferred_element_type=jnp.float32)
                * 0.125
            )
            parts.append(part if usable is None else jnp.where(usable, part, -1e30))
        top = jnp.max(parts[0], axis=-1, keepdims=True)
        for part in parts[1:]:
            top = jnp.maximum(top, jnp.max(part, axis=-1, keepdims=True))
        if carry:
            old_top = top_in[:, head * HEAD_DIM : head * HEAD_DIM + 1]
            top = jnp.maximum(top, old_top)
            scale = jnp.exp(old_top - top)
            total = total_in[:, head * HEAD_DIM : head * HEAD_DIM + 1] * scale
            mixed = mixed_in[:, lanes] * scale
        else:
            total = jnp.zeros((query.shape[0], 1), jnp.float32)
            mixed = jnp.zeros((query.shape[0], HEAD_DIM), jnp.float32)
        for part, v_ref in zip(parts, value_refs):
            probs = jnp.exp(part - top)
            total = total + jnp.sum(probs, axis=-1, keepdims=True)
            mixed = mixed + jnp.dot(
                probs.astype(jnp.bfloat16), v_ref[:, lanes], preferred_element_type=jnp.float32
            )
        tops.append(jnp.broadcast_to(top, mixed.shape))
        totals.append(jnp.broadcast_to(total, mixed.shape))
        mixes.append(mixed)
    if final:
        o_ref = rest[0]
        o_ref[...] = jnp.concatenate(
            [m / t for m, t in zip(mixes, totals)], axis=1
        ).astype(o_ref.dtype)
    else:
        rest[0][...] = jnp.concatenate(tops, axis=1)
        rest[1][...] = jnp.concatenate(totals, axis=1)
        rest[2][...] = jnp.concatenate(mixes, axis=1)


def attention(image_qkv, pieces, masks, state=None, final=True):
    rows = image_qkv.shape[0]
    pairs = HEADS // 2
    width = 2 * HEAD_DIM
    heads_width = HEADS * HEAD_DIM

    def spec(array, offset):
        return pl.BlockSpec((array.shape[0], width), lambda j: (0, j + offset))

    operands = [image_qkv]
    in_specs = [spec(image_qkv, 0)]
    for piece in pieces:
        operands += [piece, piece]
        in_specs += [spec(piece, 0), spec(piece, pairs)]
    for mask in masks:
        if mask is not None:
            operands.append(mask)
            in_specs.append(pl.BlockSpec(mask.shape, lambda j: (0, 0)))
    if state is not None:
        operands += list(state)
        in_specs += [spec(part, 0) for part in state]
    out_spec = pl.BlockSpec((rows, width), lambda j: (0, j))
    if final:
        out_specs = out_spec
        out_shape = jax.ShapeDtypeStruct((rows, heads_width), jnp.bfloat16)
    else:
        out_specs = [out_spec] * 3
        out_shape = [jax.ShapeDtypeStruct((rows, heads_width), jnp.float32)] * 3
    kernel = functools.partial(
        attention_kernel,
        masked=tuple(m is not None for m in masks),
        carry=state is not None,
        final=final,
    )
    return pl.pallas_call(
        kernel, grid=(pairs,), in_specs=in_specs, out_specs=out_specs, out_shape=out_shape
    )(*operands)


def reorder(values, cols):
    picks = jnp.arange(values.shape[1], dtype=jnp.int32)[:, None] == cols[None, :]
    return jnp.dot(values, picks.astype(values.dtype), preferred_element_type=jnp.float32).astype(
        values.dtype
    )


def per_device(
    image_tokens,
    text_tokens,
    mod_image,
    mod_text,
    text_lengths,
    item_group,
    item_step,
    step_sizes,
    guide_scales,
    qkv_weight,
    kv_weight,
    out_weight,
):
    image_rows = image_tokens.shape[1]
    text_rows = text_tokens.shape[2]
    model_width = image_tokens.shape[2]
    heads_width = HEADS * HEAD_DIM
    picture = image_tokens[0]
    mod_one = mod_image[0, 0]
    mod_two = mod_text[0, 0]

    rep_size = lax.axis_size("rep")
    seq_size = lax.axis_size("seq")
    piece_rows = qkv_weight.shape[0]
    rep_route = ("rep", rep_size, 1, False)
    z_route = ("seq", *SEQ_Z)
    route_a = (rep_route, z_route, None, ("seq", *SEQ_X), ("seq", *SEQ_Y))
    route_b = (rep_route, z_route, None, ("seq", *SEQ_Y), ("seq", *SEQ_X))
    qkv_cols = qkv_weight.shape[1]
    (packed,) = staged_gather(
        (jnp.concatenate([qkv_weight, kv_weight, out_weight.reshape(piece_rows, -1)], axis=1),),
        (route_a[:3],),
    )
    qkv_half, rest_half = staged_gather(
        (packed[:, :qkv_cols], packed[:, qkv_cols:]), (route_a[3:], route_b[3:])
    )
    qkv_half = qkv_half.reshape(-1, qkv_half.shape[-1])
    rest_half = rest_half.reshape(-1, rest_half.shape[-1])
    kv_cols = kv_weight.shape[1]
    kv_half = rest_half[:, :kv_cols]
    out_half = rest_half[:, kv_cols:].reshape(-1, out_weight.shape[1])
    cfg_index = lax.axis_index("cfg")

    def weight_scale(axis, stride):
        return stride * rep_size if axis == "seq" else stride

    source_a = route_owner(route_a, weight_scale)
    source_b = route_owner(route_b, weight_scale)

    def columns(half, rows, source):
        owner = half * (seq_size * rep_size) + source
        return (owner[:, None] * rows + jnp.arange(rows, dtype=jnp.int32)[None, :]).reshape(-1)

    own_text = text_tokens[0, 0].astype(jnp.float32)
    swapped = partner_2(jnp.concatenate([mod_one, own_text, mod_two]), "cfg", 0)
    mod_other = swapped[: mod_one.shape[0]]
    text_other = swapped[mod_one.shape[0] : mod_one.shape[0] + own_text.shape[0]]
    mod_text_other = swapped[mod_one.shape[0] + own_text.shape[0] :]

    def modulate(values, mod):
        return (layer_norm(values.astype(jnp.float32)) * (1.0 + mod[1]) + mod[0]).astype(
            jnp.bfloat16
        )

    image_mod = modulate(picture, mod_one)
    text_mod = modulate(text_tokens[0, 0], mod_two)
    image_other = modulate(picture, mod_other)
    text_other_mod = modulate(text_other, mod_text_other)
    cols_a = columns(cfg_index, piece_rows, source_a)
    cols_b = columns(cfg_index, piece_rows, source_b)

    def project(values, weight, cols):
        return jnp.dot(reorder(values, cols), weight, preferred_element_type=jnp.float32)

    sent = partner_2(
        (project(image_other, qkv_half, cols_a), project(text_other_mod, kv_half, cols_b)), "cfg", 0
    )
    qkv_total = project(image_mod, qkv_half, cols_a) + sent[0]
    kv_total = project(text_mod, kv_half, cols_b) + sent[1]
    out_other = partner_2(out_half, "cfg", 0)
    image_qkv = qkv_total.astype(jnp.bfloat16)
    text_kv = kv_total.astype(jnp.bfloat16)
    length = text_lengths[0, 0]
    image_kv = image_qkv[:, heads_width:]

    cut = 64
    filler = (-(cut + text_rows)) % 16
    local = jnp.concatenate(
        [image_kv[:cut], text_kv, jnp.zeros((filler, image_kv.shape[1]), image_kv.dtype), image_kv[cut:]]
    )
    kv_route_a = (("seq", *SEQ_Z), ("seq", *SEQ_X), ("seq", *SEQ_Y))
    kv_route_b = (("seq", *SEQ_Z), ("seq", *SEQ_Y), ("seq", *SEQ_X))
    (local,) = staged_gather((local,), (kv_route_a[:1],))
    split = cut + text_rows + filler
    part_a, part_b = staged_gather(
        (local[:, :split], local[:, split:]), (kv_route_a[1:2], kv_route_b[1:2])
    )
    pieces_a = ring_pieces(part_a, "seq", *SEQ_Y)
    pieces_b = ring_pieces(part_b, "seq", *SEQ_X)
    owners = piece_owners(
        route_owner(kv_route_a[:2], lambda axis, stride: stride),
        slot_digits("seq", *SEQ_Y) * SEQ_Y[1],
    )
    row = jnp.arange(split, dtype=jnp.int32)[None, :]
    width = image_kv.shape[1]
    masks = []
    for owner in owners:
        position = owner[:, None] * text_rows + row - cut
        valid = (row < cut) | ((row < cut + text_rows) & (position < length))
        masks.append(valid.astype(jnp.float32).reshape(1, -1))
    flat_a = [p.reshape(-1, width) for p in pieces_a]
    flat_b = [p.reshape(-1, width) for p in pieces_b]
    state = attention(image_qkv, [flat_a[0], flat_b[0]], [masks[0], None], final=False)
    state = attention(
        image_qkv,
        [flat_a[1], flat_a[4], flat_b[1], flat_b[4]],
        [masks[1], masks[4], None, None],
        state,
        final=False,
    )
    attended = attention(
        image_qkv,
        [flat_a[2], flat_a[3], flat_b[2], flat_b[3]],
        [masks[2], masks[3], None, None],
        state,
    )
    out_rows = out_weight.shape[0]
    projected = jnp.dot(
        reorder(attended, columns(cfg_index, out_rows, source_b)),
        out_half,
        preferred_element_type=jnp.float32,
    ) + jnp.dot(
        reorder(attended, columns(1 - cfg_index, out_rows, source_b)),
        out_other,
        preferred_element_type=jnp.float32,
    )
    velocity = mod_one[2] * projected
    half_width = model_width // 2
    guide_scale = jnp.sum(
        jnp.where(
            jnp.arange(guide_scales.shape[0], dtype=jnp.int32) == item_group[0], guide_scales, 0.0
        )
    )
    step_size = jnp.sum(
        jnp.where(jnp.arange(step_sizes.shape[0], dtype=jnp.int32) == item_step[0], step_sizes, 0.0)
    )
    partner = partner_2(velocity.astype(jnp.bfloat16), "cfg", 0).astype(velocity.dtype)
    cond_full = jnp.where(cfg_index == 0, velocity, partner)
    uncond_full = jnp.where(cfg_index == 0, partner, velocity)
    conditional = lax.dynamic_slice_in_dim(cond_full, cfg_index * half_width, half_width, 1)
    unconditional = lax.dynamic_slice_in_dim(uncond_full, cfg_index * half_width, half_width, 1)
    guided = unconditional + guide_scale * (conditional - unconditional)
    base_part = lax.dynamic_slice_in_dim(picture, cfg_index * half_width, half_width, 1)
    return (base_part + step_size * guided)[None]


def solution(mesh):
    placed = (
        P("rep", "seq", None),
        P("cfg", "rep", "seq", None),
        P("cfg", "rep", None, None),
        P("cfg", "rep", None, None),
        P("cfg", "rep"),
        P("rep"),
        P("rep"),
        P(),
        P(),
        P(("cfg", "seq", "rep"), None),
        P(("cfg", "seq", "rep"), None),
        P(("cfg", "seq", "rep"), None),
    )
    return jax.shard_map(
        per_device, mesh=mesh, in_specs=placed, out_specs=P("rep", "seq", "cfg"), check_vma=False
    )
```

```python
import functools

import jax
import jax.numpy as jnp
from jax import lax
from jax.sharding import PartitionSpec as P
from jax.experimental import pallas as pl

HEADS = 12
HEAD_DIM = 64


def partner_2(x, axis, apart):
    return lax.ppermute(x, axis, [(i, i ^ 1 << apart) for i in range(lax.axis_size(axis))])


def digit_shift(count, size, stride, step):
    return [
        (i, i + ((i // stride + step) % size - (i // stride) % size) * stride) for i in range(count)
    ]


def ring_gather(x, axis, size, stride, forward=True):
    count = lax.axis_size(axis)
    tmap = jax.tree.map

    def send(v, step):
        return lax.ppermute(v, axis, digit_shift(count, size, stride, step))

    if size == 1:
        return tmap(lambda v: v[None], x)
    if size == 2:
        return tmap(lambda v, w: jnp.stack([v, w]), x, send(x, 1))
    assert size == 4
    from_left = send(x, 1)
    from_right = send(x, -1)
    if forward:
        head = send(tmap(lambda v: v[: v.shape[0] // 2], from_left), 1)
        tail = send(tmap(lambda v: v[v.shape[0] // 2 :], from_right), -1)
        far = tmap(lambda u, v: jnp.concatenate([u, v]), head, tail)
    else:
        far = send(x, 2)
    return tmap(lambda *vs: jnp.stack(vs), x, from_right, far, from_left)


def ring_neighbours(x, axis, size, stride):
    count = lax.axis_size(axis)
    assert size == 4
    return (
        lax.ppermute(x, axis, digit_shift(count, size, stride, 1)),
        lax.ppermute(x, axis, digit_shift(count, size, stride, -1)),
    )


def ring_forward(from_left, from_right, axis, size, stride):
    count = lax.axis_size(axis)
    half = from_left.shape[0] // 2
    return (
        lax.ppermute(from_left[:half], axis, digit_shift(count, size, stride, 1)),
        lax.ppermute(from_right[half:], axis, digit_shift(count, size, stride, -1)),
    )


def piece_owners(prev, digits):
    half = prev.shape[0] // 2
    return [
        digits[0] + prev,
        digits[1] + prev,
        digits[2] + prev[:half],
        digits[2] + prev[half:],
        digits[3] + prev,
    ]


def slot_digits(axis, size, stride):
    own = (lax.axis_index(axis) // stride) % size
    return (own + jnp.arange(size, dtype=jnp.int32)) % size


def staged_gather(parts, routes):
    for step in range(len(routes[0])):
        parts = tuple(
            ring_gather(part, *route[step]) if route[step] else part.reshape(-1, part.shape[-1])
            for part, route in zip(parts, routes)
        )
        parts = lax.optimization_barrier(parts)
    return parts


def route_owner(route, scale):
    owner = jnp.zeros((1,), jnp.int32)
    for stage in route:
        if stage:
            axis, size, stride = stage[:3]
            digits = slot_digits(axis, size, stride) * scale(axis, stride)
            owner = (digits[:, None] + owner[None, :]).reshape(-1)
    return owner


SEQ_X = (4, 1)
SEQ_Z = (2, 4)
SEQ_Y = (4, 8)


def layer_norm(values):
    row_mean = jnp.mean(values, axis=-1, keepdims=True)
    centred = values - row_mean
    row_var = jnp.mean(centred * centred, axis=-1, keepdims=True)
    return centred / jnp.sqrt(row_var + 1e-06)


def attention_kernel(*refs, masked, carry, final):
    count = len(masked)
    q_ref = refs[0]
    key_refs = refs[1 : 1 + 2 * count : 2]
    value_refs = refs[2 : 2 + 2 * count : 2]
    rest = list(refs[1 + 2 * count :])
    masks = [rest.pop(0)[...] > 0.0 if m else None for m in masked]
    if carry:
        top_in, total_in, mixed_in = rest[0][...], rest[1][...], rest[2][...]
        rest = rest[3:]
    contract = (((1,), (1,)), ((), ()))
    tops, totals, mixes = [], [], []
    for head in range(2):
        lanes = slice(head * HEAD_DIM, (head + 1) * HEAD_DIM)
        query = q_ref[:, lanes]
        parts = []
        for k_ref, usable in zip(key_refs, masks):
            part = (
                lax.dot_general(query, k_ref[:, lanes], contract, preferred_element_type=jnp.float32)
                * 0.125
            )
            parts.append(part if usable is None else jnp.where(usable, part, -1e30))
        top = jnp.max(parts[0], axis=-1, keepdims=True)
        for part in parts[1:]:
            top = jnp.maximum(top, jnp.max(part, axis=-1, keepdims=True))
        if carry:
            old_top = top_in[:, head * HEAD_DIM : head * HEAD_DIM + 1]
            top = jnp.maximum(top, old_top)
            scale = jnp.exp(old_top - top)
            total = total_in[:, head * HEAD_DIM : head * HEAD_DIM + 1] * scale
            mixed = mixed_in[:, lanes] * scale
        else:
            total = jnp.zeros((query.shape[0], 1), jnp.float32)
            mixed = jnp.zeros((query.shape[0], HEAD_DIM), jnp.float32)
        for part, v_ref in zip(parts, value_refs):
            probs = jnp.exp(part - top)
            total = total + jnp.sum(probs, axis=-1, keepdims=True)
            mixed = mixed + jnp.dot(
                probs.astype(jnp.bfloat16), v_ref[:, lanes], preferred_element_type=jnp.float32
            )
        tops.append(jnp.broadcast_to(top, mixed.shape))
        totals.append(jnp.broadcast_to(total, mixed.shape))
        mixes.append(mixed)
    if final:
        o_ref = rest[0]
        o_ref[...] = jnp.concatenate(
            [m / t for m, t in zip(mixes, totals)], axis=1
        ).astype(o_ref.dtype)
    else:
        rest[0][...] = jnp.concatenate(tops, axis=1)
        rest[1][...] = jnp.concatenate(totals, axis=1)
        rest[2][...] = jnp.concatenate(mixes, axis=1)


def attention(image_qkv, pieces, masks, state=None, final=True):
    rows = image_qkv.shape[0]
    pairs = HEADS // 2
    width = 2 * HEAD_DIM
    heads_width = HEADS * HEAD_DIM

    def spec(array, offset):
        return pl.BlockSpec((array.shape[0], width), lambda j: (0, j + offset))

    operands = [image_qkv]
    in_specs = [spec(image_qkv, 0)]
    for piece in pieces:
        operands += [piece, piece]
        in_specs += [spec(piece, 0), spec(piece, pairs)]
    for mask in masks:
        if mask is not None:
            operands.append(mask)
            in_specs.append(pl.BlockSpec(mask.shape, lambda j: (0, 0)))
    if state is not None:
        operands += list(state)
        in_specs += [spec(part, 0) for part in state]
    out_spec = pl.BlockSpec((rows, width), lambda j: (0, j))
    if final:
        out_specs = out_spec
        out_shape = jax.ShapeDtypeStruct((rows, heads_width), jnp.bfloat16)
    else:
        out_specs = [out_spec] * 3
        out_shape = [jax.ShapeDtypeStruct((rows, heads_width), jnp.float32)] * 3
    kernel = functools.partial(
        attention_kernel,
        masked=tuple(m is not None for m in masks),
        carry=state is not None,
        final=final,
    )
    return pl.pallas_call(
        kernel, grid=(pairs,), in_specs=in_specs, out_specs=out_specs, out_shape=out_shape
    )(*operands)


def reorder(values, cols):
    picks = jnp.arange(values.shape[1], dtype=jnp.int32)[:, None] == cols[None, :]
    return jnp.dot(values, picks.astype(values.dtype), preferred_element_type=jnp.float32).astype(
        values.dtype
    )


def per_device(
    image_tokens,
    text_tokens,
    mod_image,
    mod_text,
    text_lengths,
    item_group,
    item_step,
    step_sizes,
    guide_scales,
    qkv_weight,
    kv_weight,
    out_weight,
):
    image_rows = image_tokens.shape[1]
    text_rows = text_tokens.shape[2]
    model_width = image_tokens.shape[2]
    heads_width = HEADS * HEAD_DIM
    picture = image_tokens[0]
    mod_one = mod_image[0, 0]
    mod_two = mod_text[0, 0]

    rep_size = lax.axis_size("rep")
    seq_size = lax.axis_size("seq")
    piece_rows = qkv_weight.shape[0]
    rep_route = ("rep", rep_size, 1, False)
    z_route = ("seq", *SEQ_Z)
    route_a = (rep_route, z_route, None, ("seq", *SEQ_X), ("seq", *SEQ_Y))
    route_b = (rep_route, z_route, None, ("seq", *SEQ_Y), ("seq", *SEQ_X))
    qkv_cols = qkv_weight.shape[1]
    (packed,) = staged_gather(
        (jnp.concatenate([qkv_weight, kv_weight, out_weight.reshape(piece_rows, -1)], axis=1),),
        (route_a[:3],),
    )
    qkv_half, rest_half = staged_gather(
        (packed[:, :qkv_cols], packed[:, qkv_cols:]), (route_a[3:], route_b[3:])
    )
    qkv_half = qkv_half.reshape(-1, qkv_half.shape[-1])
    rest_half = rest_half.reshape(-1, rest_half.shape[-1])
    kv_cols = kv_weight.shape[1]
    kv_half = rest_half[:, :kv_cols]
    out_half = rest_half[:, kv_cols:].reshape(-1, out_weight.shape[1])
    cfg_index = lax.axis_index("cfg")

    def weight_scale(axis, stride):
        return stride * rep_size if axis == "seq" else stride

    source_a = route_owner(route_a, weight_scale)
    source_b = route_owner(route_b, weight_scale)

    def columns(half, rows, source):
        owner = half * (seq_size * rep_size) + source
        return (owner[:, None] * rows + jnp.arange(rows, dtype=jnp.int32)[None, :]).reshape(-1)

    own_text = text_tokens[0, 0].astype(jnp.float32)
    swapped = partner_2(jnp.concatenate([mod_one, own_text, mod_two]), "cfg", 0)
    mod_other = swapped[: mod_one.shape[0]]
    text_other = swapped[mod_one.shape[0] : mod_one.shape[0] + own_text.shape[0]]
    mod_text_other = swapped[mod_one.shape[0] + own_text.shape[0] :]

    def modulate(values, mod):
        return (layer_norm(values.astype(jnp.float32)) * (1.0 + mod[1]) + mod[0]).astype(
            jnp.bfloat16
        )

    image_mod = modulate(picture, mod_one)
    text_mod = modulate(text_tokens[0, 0], mod_two)
    image_other = modulate(picture, mod_other)
    text_other_mod = modulate(text_other, mod_text_other)
    cols_a = columns(cfg_index, piece_rows, source_a)
    cols_b = columns(cfg_index, piece_rows, source_b)

    def project(values, weight, cols):
        return jnp.dot(reorder(values, cols), weight, preferred_element_type=jnp.float32)

    image_reordered = reorder(image_other, cols_a)
    key_value_cols = qkv_half[:, heads_width:]
    sent = partner_2(
        (
            jnp.dot(image_reordered, key_value_cols, preferred_element_type=jnp.float32),
            project(text_other_mod, kv_half, cols_b),
        ),
        "cfg",
        0,
    )
    sent_query = partner_2(
        jnp.dot(image_reordered, qkv_half[:, :heads_width], preferred_element_type=jnp.float32),
        "cfg",
        0,
    )
    own_reordered = reorder(image_mod, cols_a)
    key_value_total = (
        jnp.dot(own_reordered, key_value_cols, preferred_element_type=jnp.float32) + sent[0]
    )
    query_total = (
        jnp.dot(own_reordered, qkv_half[:, :heads_width], preferred_element_type=jnp.float32)
        + sent_query
    )
    kv_total = project(text_mod, kv_half, cols_b) + sent[1]
    out_other = partner_2(out_half, "cfg", 0)
    image_qkv = query_total.astype(jnp.bfloat16)
    text_kv = kv_total.astype(jnp.bfloat16)
    length = text_lengths[0, 0]
    image_kv = key_value_total.astype(jnp.bfloat16)

    cut = 64
    filler = (-(cut + text_rows)) % 16
    local = jnp.concatenate(
        [image_kv[:cut], text_kv, jnp.zeros((filler, image_kv.shape[1]), image_kv.dtype), image_kv[cut:]]
    )
    kv_route_a = (("seq", *SEQ_Z), ("seq", *SEQ_X), ("seq", *SEQ_Y))
    kv_route_b = (("seq", *SEQ_Z), ("seq", *SEQ_Y), ("seq", *SEQ_X))
    (local,) = staged_gather((local,), (kv_route_a[:1],))
    split = cut + text_rows + filler
    part_a, part_b = staged_gather(
        (local[:, :split], local[:, split:]), (kv_route_a[1:2], kv_route_b[1:2])
    )
    left_a, right_a = ring_neighbours(part_a, "seq", *SEQ_Y)
    left_b, right_b = ring_neighbours(part_b, "seq", *SEQ_X)
    owners = piece_owners(
        route_owner(kv_route_a[:2], lambda axis, stride: stride),
        slot_digits("seq", *SEQ_Y) * SEQ_Y[1],
    )
    row = jnp.arange(split, dtype=jnp.int32)[None, :]
    width = image_kv.shape[1]
    masks = []
    for owner in owners:
        position = owner[:, None] * text_rows + row - cut
        valid = (row < cut) | ((row < cut + text_rows) & (position < length))
        masks.append(valid.astype(jnp.float32).reshape(1, -1))
    def flat(p):
        return p.reshape(-1, width)

    state = attention(image_qkv, [flat(part_a), flat(part_b)], [masks[0], None], final=False)
    state, left_a, right_a, left_b, right_b = lax.optimization_barrier(
        (state, left_a, right_a, left_b, right_b)
    )
    head_a, tail_a = ring_forward(left_a, right_a, "seq", *SEQ_Y)
    head_b, tail_b = ring_forward(left_b, right_b, "seq", *SEQ_X)
    state = attention(
        image_qkv,
        [flat(right_a), flat(left_a), flat(right_b), flat(left_b)],
        [masks[1], masks[4], None, None],
        state,
        final=False,
    )
    attended = attention(
        image_qkv,
        [flat(head_a), flat(tail_a), flat(head_b), flat(tail_b)],
        [masks[2], masks[3], None, None],
        state,
    )
    out_rows = out_weight.shape[0]
    projected = jnp.dot(
        reorder(attended, columns(cfg_index, out_rows, source_b)),
        out_half,
        preferred_element_type=jnp.float32,
    ) + jnp.dot(
        reorder(attended, columns(1 - cfg_index, out_rows, source_b)),
        out_other,
        preferred_element_type=jnp.float32,
    )
    velocity = mod_one[2] * projected
    half_width = model_width // 2
    guide_scale = jnp.sum(
        jnp.where(
            jnp.arange(guide_scales.shape[0], dtype=jnp.int32) == item_group[0], guide_scales, 0.0
        )
    )
    step_size = jnp.sum(
        jnp.where(jnp.arange(step_sizes.shape[0], dtype=jnp.int32) == item_step[0], step_sizes, 0.0)
    )
    partner = partner_2(velocity.astype(jnp.bfloat16), "cfg", 0).astype(velocity.dtype)
    cond_full = jnp.where(cfg_index == 0, velocity, partner)
    uncond_full = jnp.where(cfg_index == 0, partner, velocity)
    conditional = lax.dynamic_slice_in_dim(cond_full, cfg_index * half_width, half_width, 1)
    unconditional = lax.dynamic_slice_in_dim(uncond_full, cfg_index * half_width, half_width, 1)
    guided = unconditional + guide_scale * (conditional - unconditional)
    base_part = lax.dynamic_slice_in_dim(picture, cfg_index * half_width, half_width, 1)
    return (base_part + step_size * guided)[None]


def solution(mesh):
    placed = (
        P("rep", "seq", None),
        P("cfg", "rep", "seq", None),
        P("cfg", "rep", None, None),
        P("cfg", "rep", None, None),
        P("cfg", "rep"),
        P("rep"),
        P("rep"),
        P(),
        P(),
        P(("cfg", "seq", "rep"), None),
        P(("cfg", "seq", "rep"), None),
        P(("cfg", "seq", "rep"), None),
    )
    return jax.shard_map(
        per_device, mesh=mesh, in_specs=placed, out_specs=P("rep", "seq", "cfg"), check_vma=False
    )
```

```python
import functools

import jax
import jax.numpy as jnp
from jax import lax
from jax.sharding import PartitionSpec as P
from jax.experimental import pallas as pl

HEADS = 12
HEAD_DIM = 64


def partner_2(x, axis, apart):
    return lax.ppermute(x, axis, [(i, i ^ 1 << apart) for i in range(lax.axis_size(axis))])


def digit_shift(count, size, stride, step):
    return [
        (i, i + ((i // stride + step) % size - (i // stride) % size) * stride) for i in range(count)
    ]


def ring_gather(x, axis, size, stride, forward=True):
    count = lax.axis_size(axis)
    tmap = jax.tree.map

    def send(v, step):
        return lax.ppermute(v, axis, digit_shift(count, size, stride, step))

    if size == 1:
        return tmap(lambda v: v[None], x)
    if size == 2:
        return tmap(lambda v, w: jnp.stack([v, w]), x, send(x, 1))
    assert size == 4
    from_left = send(x, 1)
    from_right = send(x, -1)
    if forward:
        head = send(tmap(lambda v: v[: v.shape[0] // 2], from_left), 1)
        tail = send(tmap(lambda v: v[v.shape[0] // 2 :], from_right), -1)
        far = tmap(lambda u, v: jnp.concatenate([u, v]), head, tail)
    else:
        far = send(x, 2)
    return tmap(lambda *vs: jnp.stack(vs), x, from_right, far, from_left)


def ring_gather_halves(x, axis, size, stride):
    count = lax.axis_size(axis)

    def send(v, step):
        return lax.ppermute(v, axis, digit_shift(count, size, stride, step))

    assert size == 4
    from_left = send(x, 1)
    from_right = send(x, -1)
    half = x.shape[0] // 2
    far = jnp.concatenate([send(from_left[:half], 1), send(from_right[half:], -1)])
    return jnp.stack([x, from_right]), jnp.stack([far, from_left])


def ring_neighbours(x, axis, size, stride):
    count = lax.axis_size(axis)
    assert size == 4
    return (
        lax.ppermute(x, axis, digit_shift(count, size, stride, 1)),
        lax.ppermute(x, axis, digit_shift(count, size, stride, -1)),
    )


def ring_forward(from_left, from_right, axis, size, stride):
    count = lax.axis_size(axis)
    half = from_left.shape[0] // 2
    return (
        lax.ppermute(from_left[:half], axis, digit_shift(count, size, stride, 1)),
        lax.ppermute(from_right[half:], axis, digit_shift(count, size, stride, -1)),
    )


def piece_owners(prev, digits):
    half = prev.shape[0] // 2
    return [
        digits[0] + prev,
        digits[1] + prev,
        digits[2] + prev[:half],
        digits[2] + prev[half:],
        digits[3] + prev,
    ]


def slot_digits(axis, size, stride):
    own = (lax.axis_index(axis) // stride) % size
    return (own + jnp.arange(size, dtype=jnp.int32)) % size


def staged_gather(parts, routes):
    for step in range(len(routes[0])):
        parts = tuple(
            ring_gather(part, *route[step]) if route[step] else part.reshape(-1, part.shape[-1])
            for part, route in zip(parts, routes)
        )
        parts = lax.optimization_barrier(parts)
    return parts


def route_owner(route, scale):
    owner = jnp.zeros((1,), jnp.int32)
    for stage in route:
        if stage:
            axis, size, stride = stage[:3]
            digits = slot_digits(axis, size, stride) * scale(axis, stride)
            owner = (digits[:, None] + owner[None, :]).reshape(-1)
    return owner


SEQ_X = (4, 1)
SEQ_Z = (2, 4)
SEQ_Y = (4, 8)


def layer_norm(values):
    row_mean = jnp.mean(values, axis=-1, keepdims=True)
    centred = values - row_mean
    row_var = jnp.mean(centred * centred, axis=-1, keepdims=True)
    return centred / jnp.sqrt(row_var + 1e-06)


def attention_kernel(*refs, masked, carry, final):
    count = len(masked)
    q_ref = refs[0]
    key_refs = refs[1 : 1 + 2 * count : 2]
    value_refs = refs[2 : 2 + 2 * count : 2]
    rest = list(refs[1 + 2 * count :])
    masks = [rest.pop(0)[...] > 0.0 if m else None for m in masked]
    if carry:
        top_in, total_in, mixed_in = rest[0][...], rest[1][...], rest[2][...]
        rest = rest[3:]
    contract = (((1,), (1,)), ((), ()))
    tops, totals, mixes = [], [], []
    for head in range(2):
        lanes = slice(head * HEAD_DIM, (head + 1) * HEAD_DIM)
        query = q_ref[:, lanes]
        parts = []
        for k_ref, usable in zip(key_refs, masks):
            part = (
                lax.dot_general(query, k_ref[:, lanes], contract, preferred_element_type=jnp.float32)
                * 0.125
            )
            parts.append(part if usable is None else jnp.where(usable, part, -1e30))
        top = jnp.max(parts[0], axis=-1, keepdims=True)
        for part in parts[1:]:
            top = jnp.maximum(top, jnp.max(part, axis=-1, keepdims=True))
        if carry:
            old_top = top_in[:, head * HEAD_DIM : head * HEAD_DIM + 1]
            top = jnp.maximum(top, old_top)
            scale = jnp.exp(old_top - top)
            total = total_in[:, head * HEAD_DIM : head * HEAD_DIM + 1] * scale
            mixed = mixed_in[:, lanes] * scale
        else:
            total = jnp.zeros((query.shape[0], 1), jnp.float32)
            mixed = jnp.zeros((query.shape[0], HEAD_DIM), jnp.float32)
        for part, v_ref in zip(parts, value_refs):
            probs = jnp.exp(part - top)
            total = total + jnp.sum(probs, axis=-1, keepdims=True)
            mixed = mixed + jnp.dot(
                probs.astype(jnp.bfloat16), v_ref[:, lanes], preferred_element_type=jnp.float32
            )
        tops.append(jnp.broadcast_to(top, mixed.shape))
        totals.append(jnp.broadcast_to(total, mixed.shape))
        mixes.append(mixed)
    if final:
        o_ref = rest[0]
        o_ref[...] = jnp.concatenate(
            [m / t for m, t in zip(mixes, totals)], axis=1
        ).astype(o_ref.dtype)
    else:
        rest[0][...] = jnp.concatenate(tops, axis=1)
        rest[1][...] = jnp.concatenate(totals, axis=1)
        rest[2][...] = jnp.concatenate(mixes, axis=1)


def attention(image_qkv, pieces, masks, state=None, final=True):
    rows = image_qkv.shape[0]
    pairs = HEADS // 2
    width = 2 * HEAD_DIM
    heads_width = HEADS * HEAD_DIM

    def spec(array, offset):
        return pl.BlockSpec((array.shape[0], width), lambda j: (0, j + offset))

    operands = [image_qkv]
    in_specs = [spec(image_qkv, 0)]
    for piece in pieces:
        operands += [piece, piece]
        in_specs += [spec(piece, 0), spec(piece, pairs)]
    for mask in masks:
        if mask is not None:
            operands.append(mask)
            in_specs.append(pl.BlockSpec(mask.shape, lambda j: (0, 0)))
    if state is not None:
        operands += list(state)
        in_specs += [spec(part, 0) for part in state]
    out_spec = pl.BlockSpec((rows, width), lambda j: (0, j))
    if final:
        out_specs = out_spec
        out_shape = jax.ShapeDtypeStruct((rows, heads_width), jnp.bfloat16)
    else:
        out_specs = [out_spec] * 3
        out_shape = [jax.ShapeDtypeStruct((rows, heads_width), jnp.float32)] * 3
    kernel = functools.partial(
        attention_kernel,
        masked=tuple(m is not None for m in masks),
        carry=state is not None,
        final=final,
    )
    return pl.pallas_call(
        kernel, grid=(pairs,), in_specs=in_specs, out_specs=out_specs, out_shape=out_shape
    )(*operands)


def reorder(values, cols):
    picks = jnp.arange(values.shape[1], dtype=jnp.int32)[:, None] == cols[None, :]
    return jnp.dot(values, picks.astype(values.dtype), preferred_element_type=jnp.float32).astype(
        values.dtype
    )


def per_device(
    image_tokens,
    text_tokens,
    mod_image,
    mod_text,
    text_lengths,
    item_group,
    item_step,
    step_sizes,
    guide_scales,
    qkv_weight,
    kv_weight,
    out_weight,
):
    image_rows = image_tokens.shape[1]
    text_rows = text_tokens.shape[2]
    model_width = image_tokens.shape[2]
    heads_width = HEADS * HEAD_DIM
    picture = image_tokens[0]
    mod_one = mod_image[0, 0]
    mod_two = mod_text[0, 0]

    rep_size = lax.axis_size("rep")
    seq_size = lax.axis_size("seq")
    piece_rows = qkv_weight.shape[0]
    rep_route = ("rep", rep_size, 1, False)
    z_route = ("seq", *SEQ_Z)
    route_a = (rep_route, z_route, None, ("seq", *SEQ_X), ("seq", *SEQ_Y))
    route_b = (rep_route, z_route, None, ("seq", *SEQ_Y), ("seq", *SEQ_X))
    qkv_cols = qkv_weight.shape[1]
    (packed,) = staged_gather(
        (jnp.concatenate([qkv_weight, kv_weight, out_weight.reshape(piece_rows, -1)], axis=1),),
        (route_a[:3],),
    )
    qkv_half, rest_half = staged_gather(
        (packed[:, :qkv_cols], packed[:, qkv_cols:]), (route_a[3:], route_b[3:])
    )
    qkv_half = qkv_half.reshape(-1, qkv_half.shape[-1])
    rest_half = rest_half.reshape(-1, rest_half.shape[-1])
    kv_cols = kv_weight.shape[1]
    kv_half = rest_half[:, :kv_cols]
    out_half = rest_half[:, kv_cols:].reshape(-1, out_weight.shape[1])
    cfg_index = lax.axis_index("cfg")

    def weight_scale(axis, stride):
        return stride * rep_size if axis == "seq" else stride

    source_a = route_owner(route_a, weight_scale)
    source_b = route_owner(route_b, weight_scale)

    def columns(half, rows, source):
        owner = half * (seq_size * rep_size) + source
        return (owner[:, None] * rows + jnp.arange(rows, dtype=jnp.int32)[None, :]).reshape(-1)

    own_text = text_tokens[0, 0].astype(jnp.float32)
    swapped = partner_2(jnp.concatenate([mod_one, own_text, mod_two]), "cfg", 0)
    mod_other = swapped[: mod_one.shape[0]]
    text_other = swapped[mod_one.shape[0] : mod_one.shape[0] + own_text.shape[0]]
    mod_text_other = swapped[mod_one.shape[0] + own_text.shape[0] :]

    def modulate(values, mod):
        return (layer_norm(values.astype(jnp.float32)) * (1.0 + mod[1]) + mod[0]).astype(
            jnp.bfloat16
        )

    image_mod = modulate(picture, mod_one)
    text_mod = modulate(text_tokens[0, 0], mod_two)
    image_other = modulate(picture, mod_other)
    text_other_mod = modulate(text_other, mod_text_other)
    cols_a = columns(cfg_index, piece_rows, source_a)
    cols_b = columns(cfg_index, piece_rows, source_b)

    def project(values, weight, cols):
        return jnp.dot(reorder(values, cols), weight, preferred_element_type=jnp.float32)

    image_reordered = reorder(image_other, cols_a)
    key_value_cols = qkv_half[:, heads_width:]
    sent = partner_2(
        (
            jnp.dot(image_reordered, key_value_cols, preferred_element_type=jnp.float32),
            project(text_other_mod, kv_half, cols_b),
        ),
        "cfg",
        0,
    )
    sent_query = partner_2(
        jnp.dot(image_reordered, qkv_half[:, :heads_width], preferred_element_type=jnp.float32),
        "cfg",
        0,
    )
    own_reordered = reorder(image_mod, cols_a)
    key_value_total = (
        jnp.dot(own_reordered, key_value_cols, preferred_element_type=jnp.float32) + sent[0]
    )
    query_total = (
        jnp.dot(own_reordered, qkv_half[:, :heads_width], preferred_element_type=jnp.float32)
        + sent_query
    )
    kv_total = project(text_mod, kv_half, cols_b) + sent[1]
    out_other = partner_2(out_half, "cfg", 0)
    image_qkv = query_total.astype(jnp.bfloat16)
    text_kv = kv_total.astype(jnp.bfloat16)
    length = text_lengths[0, 0]
    image_kv = key_value_total.astype(jnp.bfloat16)

    cut = 64
    filler = (-(cut + text_rows)) % 16
    local = jnp.concatenate(
        [image_kv[:cut], text_kv, jnp.zeros((filler, image_kv.shape[1]), image_kv.dtype), image_kv[cut:]]
    )
    kv_route_a = (("seq", *SEQ_Z), ("seq", *SEQ_X), ("seq", *SEQ_Y))
    kv_route_b = (("seq", *SEQ_Z), ("seq", *SEQ_Y), ("seq", *SEQ_X))
    (local,) = staged_gather((local,), (kv_route_a[:1],))
    split = cut + text_rows + filler
    halves = lax.optimization_barrier(
        ring_gather_halves(local[:, :split], "seq", *SEQ_X)
        + ring_gather_halves(local[:, split:], "seq", *SEQ_Y)
    )
    width = image_kv.shape[1]
    halves = [h.reshape(-1, width) for h in halves]
    axes = [SEQ_Y, SEQ_Y, SEQ_X, SEQ_X]
    from_left = [
        lax.ppermute(h, "seq", digit_shift(seq_size, *axis, 1)) for h, axis in zip(halves, axes)
    ]
    from_right = [
        lax.ppermute(h, "seq", digit_shift(seq_size, *axis, -1)) for h, axis in zip(halves, axes)
    ]
    prev = route_owner(kv_route_a[:2], lambda axis, stride: stride)
    prev = [prev[: prev.shape[0] // 2], prev[prev.shape[0] // 2 :]]
    digits = slot_digits("seq", *SEQ_Y) * SEQ_Y[1]
    row = jnp.arange(split, dtype=jnp.int32)[None, :]

    def mask(digit, owners):
        position = (digit + owners)[:, None] * text_rows + row - cut
        valid = (row < cut) | ((row < cut + text_rows) & (position < length))
        return valid.astype(jnp.float32).reshape(1, -1)

    state = attention(
        image_qkv, halves, [mask(digits[0], prev[0]), mask(digits[0], prev[1]), None, None], final=False
    )
    state, from_left, from_right = lax.optimization_barrier((state, from_left, from_right))
    forwarded = [
        lax.ppermute(from_left[0], "seq", digit_shift(seq_size, *SEQ_Y, 1)),
        lax.ppermute(from_right[1], "seq", digit_shift(seq_size, *SEQ_Y, -1)),
        lax.ppermute(from_left[2], "seq", digit_shift(seq_size, *SEQ_X, 1)),
        lax.ppermute(from_right[3], "seq", digit_shift(seq_size, *SEQ_X, -1)),
    ]
    state = attention(
        image_qkv,
        from_right + from_left,
        [mask(digits[1], prev[0]), mask(digits[1], prev[1]), None, None]
        + [mask(digits[3], prev[0]), mask(digits[3], prev[1]), None, None],
        state,
        final=False,
    )
    attended = attention(
        image_qkv, forwarded, [mask(digits[2], prev[0]), mask(digits[2], prev[1]), None, None], state
    )
    out_rows = out_weight.shape[0]
    projected = jnp.dot(
        reorder(attended, columns(cfg_index, out_rows, source_b)),
        out_half,
        preferred_element_type=jnp.float32,
    ) + jnp.dot(
        reorder(attended, columns(1 - cfg_index, out_rows, source_b)),
        out_other,
        preferred_element_type=jnp.float32,
    )
    velocity = mod_one[2] * projected
    half_width = model_width // 2
    guide_scale = jnp.sum(
        jnp.where(
            jnp.arange(guide_scales.shape[0], dtype=jnp.int32) == item_group[0], guide_scales, 0.0
        )
    )
    step_size = jnp.sum(
        jnp.where(jnp.arange(step_sizes.shape[0], dtype=jnp.int32) == item_step[0], step_sizes, 0.0)
    )
    partner = partner_2(velocity.astype(jnp.bfloat16), "cfg", 0).astype(velocity.dtype)
    cond_full = jnp.where(cfg_index == 0, velocity, partner)
    uncond_full = jnp.where(cfg_index == 0, partner, velocity)
    conditional = lax.dynamic_slice_in_dim(cond_full, cfg_index * half_width, half_width, 1)
    unconditional = lax.dynamic_slice_in_dim(uncond_full, cfg_index * half_width, half_width, 1)
    guided = unconditional + guide_scale * (conditional - unconditional)
    base_part = lax.dynamic_slice_in_dim(picture, cfg_index * half_width, half_width, 1)
    return (base_part + step_size * guided)[None]


def solution(mesh):
    placed = (
        P("rep", "seq", None),
        P("cfg", "rep", "seq", None),
        P("cfg", "rep", None, None),
        P("cfg", "rep", None, None),
        P("cfg", "rep"),
        P("rep"),
        P("rep"),
        P(),
        P(),
        P(("cfg", "seq", "rep"), None),
        P(("cfg", "seq", "rep"), None),
        P(("cfg", "seq", "rep"), None),
    )
    return jax.shard_map(
        per_device, mesh=mesh, in_specs=placed, out_specs=P("rep", "seq", "cfg"), check_vma=False
    )
```

```python
import functools

import jax
import jax.numpy as jnp
from jax import lax
from jax.sharding import PartitionSpec as P
from jax.experimental import pallas as pl

HEADS = 12
HEAD_DIM = 64


def partner_2(x, axis, apart):
    return lax.ppermute(x, axis, [(i, i ^ 1 << apart) for i in range(lax.axis_size(axis))])


def digit_shift(count, size, stride, step):
    return [
        (i, i + ((i // stride + step) % size - (i // stride) % size) * stride) for i in range(count)
    ]


def ring_gather(x, axis, size, stride, forward=True):
    count = lax.axis_size(axis)
    tmap = jax.tree.map

    def send(v, step):
        return lax.ppermute(v, axis, digit_shift(count, size, stride, step))

    if size == 1:
        return tmap(lambda v: v[None], x)
    if size == 2:
        return tmap(lambda v, w: jnp.stack([v, w]), x, send(x, 1))
    assert size == 4
    from_left = send(x, 1)
    from_right = send(x, -1)
    if forward:
        head = send(tmap(lambda v: v[: v.shape[0] // 2], from_left), 1)
        tail = send(tmap(lambda v: v[v.shape[0] // 2 :], from_right), -1)
        far = tmap(lambda u, v: jnp.concatenate([u, v]), head, tail)
    else:
        far = send(x, 2)
    return tmap(lambda *vs: jnp.stack(vs), x, from_right, far, from_left)


def ring_neighbours(x, axis, size, stride):
    count = lax.axis_size(axis)
    assert size == 4
    return (
        lax.ppermute(x, axis, digit_shift(count, size, stride, 1)),
        lax.ppermute(x, axis, digit_shift(count, size, stride, -1)),
    )


def ring_forward(from_left, from_right, axis, size, stride):
    count = lax.axis_size(axis)
    half = from_left.shape[0] // 2
    return (
        lax.ppermute(from_left[:half], axis, digit_shift(count, size, stride, 1)),
        lax.ppermute(from_right[half:], axis, digit_shift(count, size, stride, -1)),
    )


def piece_owners(prev, digits):
    half = prev.shape[0] // 2
    return [
        digits[0] + prev,
        digits[1] + prev,
        digits[2] + prev[:half],
        digits[2] + prev[half:],
        digits[3] + prev,
    ]


def slot_digits(axis, size, stride):
    own = (lax.axis_index(axis) // stride) % size
    return (own + jnp.arange(size, dtype=jnp.int32)) % size


def staged_gather(parts, routes):
    for step in range(len(routes[0])):
        parts = tuple(
            ring_gather(part, *route[step]) if route[step] else part.reshape(-1, part.shape[-1])
            for part, route in zip(parts, routes)
        )
        parts = lax.optimization_barrier(parts)
    return parts


def route_owner(route, scale):
    owner = jnp.zeros((1,), jnp.int32)
    for stage in route:
        if stage:
            axis, size, stride = stage[:3]
            digits = slot_digits(axis, size, stride) * scale(axis, stride)
            owner = (digits[:, None] + owner[None, :]).reshape(-1)
    return owner


SEQ_X = (4, 1)
SEQ_Z = (2, 4)
SEQ_Y = (4, 8)


def layer_norm(values):
    row_mean = jnp.mean(values, axis=-1, keepdims=True)
    centred = values - row_mean
    row_var = jnp.mean(centred * centred, axis=-1, keepdims=True)
    return centred / jnp.sqrt(row_var + 1e-06)


def attention_kernel(*refs, masked, carry, final):
    count = len(masked)
    q_ref = refs[0]
    key_refs = refs[1 : 1 + 2 * count : 2]
    value_refs = refs[2 : 2 + 2 * count : 2]
    rest = list(refs[1 + 2 * count :])
    masks = [rest.pop(0)[...] > 0.0 if m else None for m in masked]
    if carry:
        top_in, total_in, mixed_in = rest[0][...], rest[1][...], rest[2][...]
        rest = rest[3:]
    contract = (((1,), (1,)), ((), ()))
    tops, totals, mixes = [], [], []
    for head in range(q_ref.shape[1] // HEAD_DIM):
        lanes = slice(head * HEAD_DIM, (head + 1) * HEAD_DIM)
        query = q_ref[:, lanes]
        parts = []
        for k_ref, usable in zip(key_refs, masks):
            part = (
                lax.dot_general(query, k_ref[:, lanes], contract, preferred_element_type=jnp.float32)
                * 0.125
            )
            parts.append(part if usable is None else jnp.where(usable, part, -1e30))
        top = jnp.max(parts[0], axis=-1, keepdims=True)
        for part in parts[1:]:
            top = jnp.maximum(top, jnp.max(part, axis=-1, keepdims=True))
        if carry:
            old_top = top_in[:, head * HEAD_DIM : head * HEAD_DIM + 1]
            top = jnp.maximum(top, old_top)
            scale = jnp.exp(old_top - top)
            total = total_in[:, head * HEAD_DIM : head * HEAD_DIM + 1] * scale
            mixed = mixed_in[:, lanes] * scale
        else:
            total = jnp.zeros((query.shape[0], 1), jnp.float32)
            mixed = jnp.zeros((query.shape[0], HEAD_DIM), jnp.float32)
        for part, v_ref in zip(parts, value_refs):
            probs = jnp.exp(part - top)
            total = total + jnp.sum(probs, axis=-1, keepdims=True)
            mixed = mixed + jnp.dot(
                probs.astype(jnp.bfloat16), v_ref[:, lanes], preferred_element_type=jnp.float32
            )
        tops.append(jnp.broadcast_to(top, mixed.shape))
        totals.append(jnp.broadcast_to(total, mixed.shape))
        mixes.append(mixed)
    if final:
        o_ref = rest[0]
        o_ref[...] = jnp.concatenate(
            [m / t for m, t in zip(mixes, totals)], axis=1
        ).astype(o_ref.dtype)
    else:
        rest[0][...] = jnp.concatenate(tops, axis=1)
        rest[1][...] = jnp.concatenate(totals, axis=1)
        rest[2][...] = jnp.concatenate(mixes, axis=1)


def attention(image_qkv, pieces, masks, state=None, final=True):
    rows = image_qkv.shape[0]
    pairs = HEADS // 4
    width = 4 * HEAD_DIM
    heads_width = HEADS * HEAD_DIM

    def spec(array, offset):
        return pl.BlockSpec((array.shape[0], width), lambda j: (0, j + offset))

    operands = [image_qkv]
    in_specs = [spec(image_qkv, 0)]
    for piece in pieces:
        operands += [piece, piece]
        in_specs += [spec(piece, 0), spec(piece, pairs)]
    for mask in masks:
        if mask is not None:
            operands.append(mask)
            in_specs.append(pl.BlockSpec(mask.shape, lambda j: (0, 0)))
    if state is not None:
        operands += list(state)
        in_specs += [spec(part, 0) for part in state]
    out_spec = pl.BlockSpec((rows, width), lambda j: (0, j))
    if final:
        out_specs = out_spec
        out_shape = jax.ShapeDtypeStruct((rows, heads_width), jnp.bfloat16)
    else:
        out_specs = [out_spec] * 3
        out_shape = [jax.ShapeDtypeStruct((rows, heads_width), jnp.float32)] * 3
    kernel = functools.partial(
        attention_kernel,
        masked=tuple(m is not None for m in masks),
        carry=state is not None,
        final=final,
    )
    return pl.pallas_call(
        kernel, grid=(pairs,), in_specs=in_specs, out_specs=out_specs, out_shape=out_shape
    )(*operands)


def reorder(values, cols):
    picks = jnp.arange(values.shape[1], dtype=jnp.int32)[:, None] == cols[None, :]
    return jnp.dot(values, picks.astype(values.dtype), preferred_element_type=jnp.float32).astype(
        values.dtype
    )


def per_device(
    image_tokens,
    text_tokens,
    mod_image,
    mod_text,
    text_lengths,
    item_group,
    item_step,
    step_sizes,
    guide_scales,
    qkv_weight,
    kv_weight,
    out_weight,
):
    image_rows = image_tokens.shape[1]
    text_rows = text_tokens.shape[2]
    model_width = image_tokens.shape[2]
    heads_width = HEADS * HEAD_DIM
    picture = image_tokens[0]
    mod_one = mod_image[0, 0]
    mod_two = mod_text[0, 0]

    rep_size = lax.axis_size("rep")
    seq_size = lax.axis_size("seq")
    piece_rows = qkv_weight.shape[0]
    rep_route = ("rep", rep_size, 1, False)
    z_route = ("seq", *SEQ_Z)
    route_a = (rep_route, z_route, None, ("seq", *SEQ_X), ("seq", *SEQ_Y))
    route_b = (rep_route, z_route, None, ("seq", *SEQ_Y), ("seq", *SEQ_X))
    qkv_cols = qkv_weight.shape[1]
    (packed,) = staged_gather(
        (jnp.concatenate([qkv_weight, kv_weight, out_weight.reshape(piece_rows, -1)], axis=1),),
        (route_a[:3],),
    )
    qkv_half, rest_half = staged_gather(
        (packed[:, :qkv_cols], packed[:, qkv_cols:]), (route_a[3:], route_b[3:])
    )
    qkv_half = qkv_half.reshape(-1, qkv_half.shape[-1])
    rest_half = rest_half.reshape(-1, rest_half.shape[-1])
    kv_cols = kv_weight.shape[1]
    kv_half = rest_half[:, :kv_cols]
    out_half = rest_half[:, kv_cols:].reshape(-1, out_weight.shape[1])
    cfg_index = lax.axis_index("cfg")

    def weight_scale(axis, stride):
        return stride * rep_size if axis == "seq" else stride

    source_a = route_owner(route_a, weight_scale)
    source_b = route_owner(route_b, weight_scale)

    def columns(half, rows, source):
        owner = half * (seq_size * rep_size) + source
        return (owner[:, None] * rows + jnp.arange(rows, dtype=jnp.int32)[None, :]).reshape(-1)

    own_text = text_tokens[0, 0].astype(jnp.float32)
    swapped = partner_2(jnp.concatenate([mod_one, own_text, mod_two]), "cfg", 0)
    mod_other = swapped[: mod_one.shape[0]]
    text_other = swapped[mod_one.shape[0] : mod_one.shape[0] + own_text.shape[0]]
    mod_text_other = swapped[mod_one.shape[0] + own_text.shape[0] :]

    def modulate(values, mod):
        return (layer_norm(values.astype(jnp.float32)) * (1.0 + mod[1]) + mod[0]).astype(
            jnp.bfloat16
        )

    image_mod = modulate(picture, mod_one)
    text_mod = modulate(text_tokens[0, 0], mod_two)
    image_other = modulate(picture, mod_other)
    text_other_mod = modulate(text_other, mod_text_other)
    cols_a = columns(cfg_index, piece_rows, source_a)
    cols_b = columns(cfg_index, piece_rows, source_b)

    def project(values, weight, cols):
        return jnp.dot(reorder(values, cols), weight, preferred_element_type=jnp.float32)

    image_reordered = reorder(image_other, cols_a)
    key_value_cols = qkv_half[:, heads_width:]
    sent = partner_2(
        (
            jnp.dot(image_reordered, key_value_cols, preferred_element_type=jnp.float32),
            project(text_other_mod, kv_half, cols_b),
        ),
        "cfg",
        0,
    )
    sent_query = partner_2(
        jnp.dot(image_reordered, qkv_half[:, :heads_width], preferred_element_type=jnp.float32),
        "cfg",
        0,
    )
    own_reordered = reorder(image_mod, cols_a)
    key_value_total = (
        jnp.dot(own_reordered, key_value_cols, preferred_element_type=jnp.float32) + sent[0]
    )
    query_total = (
        jnp.dot(own_reordered, qkv_half[:, :heads_width], preferred_element_type=jnp.float32)
        + sent_query
    )
    kv_total = project(text_mod, kv_half, cols_b) + sent[1]
    out_other = partner_2(out_half, "cfg", 0)
    image_qkv = query_total.astype(jnp.bfloat16)
    text_kv = kv_total.astype(jnp.bfloat16)
    length = text_lengths[0, 0]
    image_kv = key_value_total.astype(jnp.bfloat16)

    cut = 64
    filler = (-(cut + text_rows)) % 16
    local = jnp.concatenate(
        [image_kv[:cut], text_kv, jnp.zeros((filler, image_kv.shape[1]), image_kv.dtype), image_kv[cut:]]
    )
    kv_route_a = (("seq", *SEQ_Z), ("seq", *SEQ_X), ("seq", *SEQ_Y))
    kv_route_b = (("seq", *SEQ_Z), ("seq", *SEQ_Y), ("seq", *SEQ_X))
    (local,) = staged_gather((local,), (kv_route_a[:1],))
    split = cut + text_rows + filler
    part_a, part_b = staged_gather(
        (local[:, :split], local[:, split:]), (kv_route_a[1:2], kv_route_b[1:2])
    )
    left_a, right_a = ring_neighbours(part_a, "seq", *SEQ_Y)
    left_b, right_b = ring_neighbours(part_b, "seq", *SEQ_X)
    owners = piece_owners(
        route_owner(kv_route_a[:2], lambda axis, stride: stride),
        slot_digits("seq", *SEQ_Y) * SEQ_Y[1],
    )
    row = jnp.arange(split, dtype=jnp.int32)[None, :]
    width = image_kv.shape[1]
    masks = []
    for owner in owners:
        position = owner[:, None] * text_rows + row - cut
        valid = (row < cut) | ((row < cut + text_rows) & (position < length))
        masks.append(valid.astype(jnp.float32).reshape(1, -1))
    def flat(p):
        return p.reshape(-1, width)

    state = attention(image_qkv, [flat(part_a), flat(part_b)], [masks[0], None], final=False)
    state, left_a, right_a, left_b, right_b = lax.optimization_barrier(
        (state, left_a, right_a, left_b, right_b)
    )
    head_a, tail_a = ring_forward(left_a, right_a, "seq", *SEQ_Y)
    head_b, tail_b = ring_forward(left_b, right_b, "seq", *SEQ_X)
    state = attention(
        image_qkv,
        [flat(right_a), flat(left_a), flat(right_b), flat(left_b)],
        [masks[1], masks[4], None, None],
        state,
        final=False,
    )
    attended = attention(
        image_qkv,
        [flat(head_a), flat(tail_a), flat(head_b), flat(tail_b)],
        [masks[2], masks[3], None, None],
        state,
    )
    out_rows = out_weight.shape[0]
    projected = jnp.dot(
        reorder(attended, columns(cfg_index, out_rows, source_b)),
        out_half,
        preferred_element_type=jnp.float32,
    ) + jnp.dot(
        reorder(attended, columns(1 - cfg_index, out_rows, source_b)),
        out_other,
        preferred_element_type=jnp.float32,
    )
    velocity = mod_one[2] * projected
    half_width = model_width // 2
    guide_scale = jnp.sum(
        jnp.where(
            jnp.arange(guide_scales.shape[0], dtype=jnp.int32) == item_group[0], guide_scales, 0.0
        )
    )
    step_size = jnp.sum(
        jnp.where(jnp.arange(step_sizes.shape[0], dtype=jnp.int32) == item_step[0], step_sizes, 0.0)
    )
    partner = partner_2(velocity.astype(jnp.bfloat16), "cfg", 0).astype(velocity.dtype)
    cond_full = jnp.where(cfg_index == 0, velocity, partner)
    uncond_full = jnp.where(cfg_index == 0, partner, velocity)
    conditional = lax.dynamic_slice_in_dim(cond_full, cfg_index * half_width, half_width, 1)
    unconditional = lax.dynamic_slice_in_dim(uncond_full, cfg_index * half_width, half_width, 1)
    guided = unconditional + guide_scale * (conditional - unconditional)
    base_part = lax.dynamic_slice_in_dim(picture, cfg_index * half_width, half_width, 1)
    return (base_part + step_size * guided)[None]


def solution(mesh):
    placed = (
        P("rep", "seq", None),
        P("cfg", "rep", "seq", None),
        P("cfg", "rep", None, None),
        P("cfg", "rep", None, None),
        P("cfg", "rep"),
        P("rep"),
        P("rep"),
        P(),
        P(),
        P(("cfg", "seq", "rep"), None),
        P(("cfg", "seq", "rep"), None),
        P(("cfg", "seq", "rep"), None),
    )
    return jax.shard_map(
        per_device, mesh=mesh, in_specs=placed, out_specs=P("rep", "seq", "cfg"), check_vma=False
    )
```

```python
import functools

import jax
import jax.numpy as jnp
from jax import lax
from jax.sharding import PartitionSpec as P
from jax.experimental import pallas as pl

HEADS = 12
HEAD_DIM = 64


def partner_2(x, axis, apart):
    return lax.ppermute(x, axis, [(i, i ^ 1 << apart) for i in range(lax.axis_size(axis))])


def digit_shift(count, size, stride, step):
    return [
        (i, i + ((i // stride + step) % size - (i // stride) % size) * stride) for i in range(count)
    ]


def ring_gather(x, axis, size, stride, forward=True):
    count = lax.axis_size(axis)
    tmap = jax.tree.map

    def send(v, step):
        return lax.ppermute(v, axis, digit_shift(count, size, stride, step))

    if size == 1:
        return tmap(lambda v: v[None], x)
    if size == 2:
        return tmap(lambda v, w: jnp.stack([v, w]), x, send(x, 1))
    assert size == 4
    from_left = send(x, 1)
    from_right = send(x, -1)
    if forward:
        head = send(tmap(lambda v: v[: v.shape[0] // 2], from_left), 1)
        tail = send(tmap(lambda v: v[v.shape[0] // 2 :], from_right), -1)
        far = tmap(lambda u, v: jnp.concatenate([u, v]), head, tail)
    else:
        far = send(x, 2)
    return tmap(lambda *vs: jnp.stack(vs), x, from_right, far, from_left)


def ring_neighbours(x, axis, size, stride):
    count = lax.axis_size(axis)
    assert size == 4
    return (
        lax.ppermute(x, axis, digit_shift(count, size, stride, 1)),
        lax.ppermute(x, axis, digit_shift(count, size, stride, -1)),
    )


def ring_forward(from_left, from_right, axis, size, stride):
    count = lax.axis_size(axis)
    half = from_left.shape[0] // 2
    return (
        lax.ppermute(from_left[:half], axis, digit_shift(count, size, stride, 1)),
        lax.ppermute(from_right[half:], axis, digit_shift(count, size, stride, -1)),
    )


def piece_owners(prev, digits):
    half = prev.shape[0] // 2
    return [
        digits[0] + prev,
        digits[1] + prev,
        digits[2] + prev[:half],
        digits[2] + prev[half:],
        digits[3] + prev,
    ]


def slot_digits(axis, size, stride):
    own = (lax.axis_index(axis) // stride) % size
    return (own + jnp.arange(size, dtype=jnp.int32)) % size


def staged_gather(parts, routes):
    for step in range(len(routes[0])):
        parts = tuple(
            ring_gather(part, *route[step]) if route[step] else part.reshape(-1, part.shape[-1])
            for part, route in zip(parts, routes)
        )
        parts = lax.optimization_barrier(parts)
    return parts


def route_owner(route, scale):
    owner = jnp.zeros((1,), jnp.int32)
    for stage in route:
        if stage:
            axis, size, stride = stage[:3]
            digits = slot_digits(axis, size, stride) * scale(axis, stride)
            owner = (digits[:, None] + owner[None, :]).reshape(-1)
    return owner


SEQ_X = (4, 1)
SEQ_Z = (2, 4)
SEQ_Y = (4, 8)


def layer_norm(values):
    row_mean = jnp.mean(values, axis=-1, keepdims=True)
    centred = values - row_mean
    row_var = jnp.mean(centred * centred, axis=-1, keepdims=True)
    return centred / jnp.sqrt(row_var + 1e-06)


def attention_kernel(*refs, masked, carry, final):
    count = len(masked)
    q_ref = refs[0]
    key_refs = refs[1 : 1 + 2 * count : 2]
    value_refs = refs[2 : 2 + 2 * count : 2]
    rest = list(refs[1 + 2 * count :])
    masks = [rest.pop(0)[...] > 0.0 if m else None for m in masked]
    if carry:
        top_in, total_in, mixed_in = rest[0][...], rest[1][...], rest[2][...]
        rest = rest[3:]
    contract = (((1,), (1,)), ((), ()))
    tops, totals, mixes = [], [], []
    for head in range(q_ref.shape[1] // HEAD_DIM):
        lanes = slice(head * HEAD_DIM, (head + 1) * HEAD_DIM)
        query = q_ref[:, lanes]
        parts = []
        for k_ref, usable in zip(key_refs, masks):
            part = (
                lax.dot_general(query, k_ref[:, lanes], contract, preferred_element_type=jnp.float32)
                * 0.125
            )
            parts.append(part if usable is None else jnp.where(usable, part, -1e30))
        top = jnp.max(parts[0], axis=-1, keepdims=True)
        for part in parts[1:]:
            top = jnp.maximum(top, jnp.max(part, axis=-1, keepdims=True))
        if carry:
            old_top = top_in[:, head * HEAD_DIM : head * HEAD_DIM + 1]
            top = jnp.maximum(top, old_top)
            scale = jnp.exp(old_top - top)
            total = total_in[:, head * HEAD_DIM : head * HEAD_DIM + 1] * scale
            mixed = mixed_in[:, lanes] * scale
        else:
            total = jnp.zeros((query.shape[0], 1), jnp.float32)
            mixed = jnp.zeros((query.shape[0], HEAD_DIM), jnp.float32)
        for part, v_ref in zip(parts, value_refs):
            probs = jnp.exp(part - top)
            total = total + jnp.sum(probs, axis=-1, keepdims=True)
            mixed = mixed + jnp.dot(
                probs.astype(jnp.bfloat16), v_ref[:, lanes], preferred_element_type=jnp.float32
            )
        tops.append(jnp.broadcast_to(top, mixed.shape))
        totals.append(jnp.broadcast_to(total, mixed.shape))
        mixes.append(mixed)
    if final:
        o_ref = rest[0]
        o_ref[...] = jnp.concatenate(
            [m / t for m, t in zip(mixes, totals)], axis=1
        ).astype(o_ref.dtype)
    else:
        rest[0][...] = jnp.concatenate(tops, axis=1)
        rest[1][...] = jnp.concatenate(totals, axis=1)
        rest[2][...] = jnp.concatenate(mixes, axis=1)


def attention(image_qkv, pieces, masks, state=None, final=True):
    rows = image_qkv.shape[0]
    pairs = HEADS // 4
    width = 4 * HEAD_DIM
    heads_width = HEADS * HEAD_DIM

    def spec(array, offset):
        return pl.BlockSpec((array.shape[0], width), lambda j: (0, j + offset))

    operands = [image_qkv]
    in_specs = [spec(image_qkv, 0)]
    for piece in pieces:
        operands += [piece, piece]
        in_specs += [spec(piece, 0), spec(piece, pairs)]
    for mask in masks:
        if mask is not None:
            operands.append(mask)
            in_specs.append(pl.BlockSpec(mask.shape, lambda j: (0, 0)))
    if state is not None:
        operands += list(state)
        in_specs += [spec(part, 0) for part in state]
    out_spec = pl.BlockSpec((rows, width), lambda j: (0, j))
    if final:
        out_specs = out_spec
        out_shape = jax.ShapeDtypeStruct((rows, heads_width), jnp.bfloat16)
    else:
        out_specs = [out_spec] * 3
        out_shape = [jax.ShapeDtypeStruct((rows, heads_width), jnp.float32)] * 3
    kernel = functools.partial(
        attention_kernel,
        masked=tuple(m is not None for m in masks),
        carry=state is not None,
        final=final,
    )
    return pl.pallas_call(
        kernel, grid=(pairs,), in_specs=in_specs, out_specs=out_specs, out_shape=out_shape
    )(*operands)


def reorder(values, cols):
    picks = jnp.arange(values.shape[1], dtype=jnp.int32)[:, None] == cols[None, :]
    return jnp.dot(values, picks.astype(values.dtype), preferred_element_type=jnp.float32).astype(
        values.dtype
    )


def per_device(
    image_tokens,
    text_tokens,
    mod_image,
    mod_text,
    text_lengths,
    item_group,
    item_step,
    step_sizes,
    guide_scales,
    qkv_weight,
    kv_weight,
    out_weight,
):
    image_rows = image_tokens.shape[1]
    text_rows = text_tokens.shape[2]
    model_width = image_tokens.shape[2]
    heads_width = HEADS * HEAD_DIM
    picture = image_tokens[0]
    mod_one = mod_image[0, 0]
    mod_two = mod_text[0, 0]

    rep_size = lax.axis_size("rep")
    seq_size = lax.axis_size("seq")
    piece_rows = qkv_weight.shape[0]
    rep_route = ("rep", rep_size, 1, False)
    z_route = ("seq", *SEQ_Z)
    route_a = (rep_route, z_route, None, ("seq", *SEQ_X, False), ("seq", *SEQ_Y))
    route_b = (rep_route, z_route, None, ("seq", *SEQ_Y, False), ("seq", *SEQ_X))
    qkv_cols = qkv_weight.shape[1]
    (packed,) = staged_gather(
        (jnp.concatenate([qkv_weight, kv_weight, out_weight.reshape(piece_rows, -1)], axis=1),),
        (route_a[:3],),
    )
    qkv_half, rest_half = staged_gather(
        (packed[:, :qkv_cols], packed[:, qkv_cols:]), (route_a[3:], route_b[3:])
    )
    qkv_half = qkv_half.reshape(-1, qkv_half.shape[-1])
    rest_half = rest_half.reshape(-1, rest_half.shape[-1])
    kv_cols = kv_weight.shape[1]
    kv_half = rest_half[:, :kv_cols]
    out_half = rest_half[:, kv_cols:].reshape(-1, out_weight.shape[1])
    cfg_index = lax.axis_index("cfg")

    def weight_scale(axis, stride):
        return stride * rep_size if axis == "seq" else stride

    source_a = route_owner(route_a, weight_scale)
    source_b = route_owner(route_b, weight_scale)

    def columns(half, rows, source):
        owner = half * (seq_size * rep_size) + source
        return (owner[:, None] * rows + jnp.arange(rows, dtype=jnp.int32)[None, :]).reshape(-1)

    own_text = text_tokens[0, 0].astype(jnp.float32)
    swapped = partner_2(jnp.concatenate([mod_one, own_text, mod_two]), "cfg", 0)
    mod_other = swapped[: mod_one.shape[0]]
    text_other = swapped[mod_one.shape[0] : mod_one.shape[0] + own_text.shape[0]]
    mod_text_other = swapped[mod_one.shape[0] + own_text.shape[0] :]

    def modulate(values, mod):
        return (layer_norm(values.astype(jnp.float32)) * (1.0 + mod[1]) + mod[0]).astype(
            jnp.bfloat16
        )

    image_mod = modulate(picture, mod_one)
    text_mod = modulate(text_tokens[0, 0], mod_two)
    image_other = modulate(picture, mod_other)
    text_other_mod = modulate(text_other, mod_text_other)
    cols_a = columns(cfg_index, piece_rows, source_a)
    cols_b = columns(cfg_index, piece_rows, source_b)

    def project(values, weight, cols):
        return jnp.dot(reorder(values, cols), weight, preferred_element_type=jnp.float32)

    image_reordered = reorder(image_other, cols_a)
    key_value_cols = qkv_half[:, heads_width:]
    sent = partner_2(
        (
            jnp.dot(image_reordered, key_value_cols, preferred_element_type=jnp.float32),
            project(text_other_mod, kv_half, cols_b),
        ),
        "cfg",
        0,
    )
    sent_query = partner_2(
        jnp.dot(image_reordered, qkv_half[:, :heads_width], preferred_element_type=jnp.float32),
        "cfg",
        0,
    )
    own_reordered = reorder(image_mod, cols_a)
    key_value_total = (
        jnp.dot(own_reordered, key_value_cols, preferred_element_type=jnp.float32) + sent[0]
    )
    query_total = (
        jnp.dot(own_reordered, qkv_half[:, :heads_width], preferred_element_type=jnp.float32)
        + sent_query
    )
    kv_total = project(text_mod, kv_half, cols_b) + sent[1]
    out_other = partner_2(out_half, "cfg", 0)
    image_qkv = query_total.astype(jnp.bfloat16)
    text_kv = kv_total.astype(jnp.bfloat16)
    length = text_lengths[0, 0]
    image_kv = key_value_total.astype(jnp.bfloat16)

    cut = 64
    filler = (-(cut + text_rows)) % 16
    local = jnp.concatenate(
        [image_kv[:cut], text_kv, jnp.zeros((filler, image_kv.shape[1]), image_kv.dtype), image_kv[cut:]]
    )
    kv_route_a = (("seq", *SEQ_Z), ("seq", *SEQ_X, False), ("seq", *SEQ_Y))
    kv_route_b = (("seq", *SEQ_Z), ("seq", *SEQ_Y, False), ("seq", *SEQ_X))
    (local,) = staged_gather((local,), (kv_route_a[:1],))
    split = cut + text_rows + filler
    part_a, part_b = staged_gather(
        (local[:, :split], local[:, split:]), (kv_route_a[1:2], kv_route_b[1:2])
    )
    left_a, right_a = ring_neighbours(part_a, "seq", *SEQ_Y)
    left_b, right_b = ring_neighbours(part_b, "seq", *SEQ_X)
    owners = piece_owners(
        route_owner(kv_route_a[:2], lambda axis, stride: stride),
        slot_digits("seq", *SEQ_Y) * SEQ_Y[1],
    )
    row = jnp.arange(split, dtype=jnp.int32)[None, :]
    width = image_kv.shape[1]
    masks = []
    for owner in owners:
        position = owner[:, None] * text_rows + row - cut
        valid = (row < cut) | ((row < cut + text_rows) & (position < length))
        masks.append(valid.astype(jnp.float32).reshape(1, -1))
    def flat(p):
        return p.reshape(-1, width)

    state = attention(image_qkv, [flat(part_a), flat(part_b)], [masks[0], None], final=False)
    state, left_a, right_a, left_b, right_b = lax.optimization_barrier(
        (state, left_a, right_a, left_b, right_b)
    )
    head_a, tail_a = ring_forward(left_a, right_a, "seq", *SEQ_Y)
    head_b, tail_b = ring_forward(left_b, right_b, "seq", *SEQ_X)
    state = attention(
        image_qkv,
        [flat(right_a), flat(left_a), flat(right_b), flat(left_b)],
        [masks[1], masks[4], None, None],
        state,
        final=False,
    )
    attended = attention(
        image_qkv,
        [flat(head_a), flat(tail_a), flat(head_b), flat(tail_b)],
        [masks[2], masks[3], None, None],
        state,
    )
    out_rows = out_weight.shape[0]
    projected = jnp.dot(
        reorder(attended, columns(cfg_index, out_rows, source_b)),
        out_half,
        preferred_element_type=jnp.float32,
    ) + jnp.dot(
        reorder(attended, columns(1 - cfg_index, out_rows, source_b)),
        out_other,
        preferred_element_type=jnp.float32,
    )
    velocity = mod_one[2] * projected
    half_width = model_width // 2
    guide_scale = jnp.sum(
        jnp.where(
            jnp.arange(guide_scales.shape[0], dtype=jnp.int32) == item_group[0], guide_scales, 0.0
        )
    )
    step_size = jnp.sum(
        jnp.where(jnp.arange(step_sizes.shape[0], dtype=jnp.int32) == item_step[0], step_sizes, 0.0)
    )
    partner = partner_2(velocity.astype(jnp.bfloat16), "cfg", 0).astype(velocity.dtype)
    cond_full = jnp.where(cfg_index == 0, velocity, partner)
    uncond_full = jnp.where(cfg_index == 0, partner, velocity)
    conditional = lax.dynamic_slice_in_dim(cond_full, cfg_index * half_width, half_width, 1)
    unconditional = lax.dynamic_slice_in_dim(uncond_full, cfg_index * half_width, half_width, 1)
    guided = unconditional + guide_scale * (conditional - unconditional)
    base_part = lax.dynamic_slice_in_dim(picture, cfg_index * half_width, half_width, 1)
    return (base_part + step_size * guided)[None]


def solution(mesh):
    placed = (
        P("rep", "seq", None),
        P("cfg", "rep", "seq", None),
        P("cfg", "rep", None, None),
        P("cfg", "rep", None, None),
        P("cfg", "rep"),
        P("rep"),
        P("rep"),
        P(),
        P(),
        P(("cfg", "seq", "rep"), None),
        P(("cfg", "seq", "rep"), None),
        P(("cfg", "seq", "rep"), None),
    )
    return jax.shard_map(
        per_device, mesh=mesh, in_specs=placed, out_specs=P("rep", "seq", "cfg"), check_vma=False
    )
```

```python
import functools

import jax
import jax.numpy as jnp
from jax import lax
from jax.sharding import PartitionSpec as P
from jax.experimental import pallas as pl

HEADS = 12
HEAD_DIM = 64


def partner_2(x, axis, apart):
    return lax.ppermute(x, axis, [(i, i ^ 1 << apart) for i in range(lax.axis_size(axis))])


def digit_shift(count, size, stride, step):
    return [
        (i, i + ((i // stride + step) % size - (i // stride) % size) * stride) for i in range(count)
    ]


def ring_gather(x, axis, size, stride, forward=True):
    count = lax.axis_size(axis)
    tmap = jax.tree.map

    def send(v, step):
        return lax.ppermute(v, axis, digit_shift(count, size, stride, step))

    if size == 1:
        return tmap(lambda v: v[None], x)
    if size == 2:
        return tmap(lambda v, w: jnp.stack([v, w]), x, send(x, 1))
    assert size == 4
    from_left = send(x, 1)
    from_right = send(x, -1)
    if forward:
        head = send(tmap(lambda v: v[: v.shape[0] // 2], from_left), 1)
        tail = send(tmap(lambda v: v[v.shape[0] // 2 :], from_right), -1)
        far = tmap(lambda u, v: jnp.concatenate([u, v]), head, tail)
    else:
        far = send(x, 2)
    return tmap(lambda *vs: jnp.stack(vs), x, from_right, far, from_left)


def ring_neighbours(x, axis, size, stride):
    count = lax.axis_size(axis)
    assert size == 4
    return (
        lax.ppermute(x, axis, digit_shift(count, size, stride, 1)),
        lax.ppermute(x, axis, digit_shift(count, size, stride, -1)),
    )


def ring_forward(from_left, from_right, axis, size, stride):
    count = lax.axis_size(axis)
    half = from_left.shape[0] // 2
    return (
        lax.ppermute(from_left[:half], axis, digit_shift(count, size, stride, 1)),
        lax.ppermute(from_right[half:], axis, digit_shift(count, size, stride, -1)),
    )


def piece_owners(prev, digits):
    half = prev.shape[0] // 2
    return [
        digits[0] + prev,
        digits[1] + prev,
        digits[2] + prev[:half],
        digits[2] + prev[half:],
        digits[3] + prev,
    ]


def slot_digits(axis, size, stride):
    own = (lax.axis_index(axis) // stride) % size
    return (own + jnp.arange(size, dtype=jnp.int32)) % size


def staged_gather(parts, routes):
    for step in range(len(routes[0])):
        parts = tuple(
            ring_gather(part, *route[step]) if route[step] else part.reshape(-1, part.shape[-1])
            for part, route in zip(parts, routes)
        )
        parts = lax.optimization_barrier(parts)
    return parts


def route_owner(route, scale):
    owner = jnp.zeros((1,), jnp.int32)
    for stage in route:
        if stage:
            axis, size, stride = stage[:3]
            digits = slot_digits(axis, size, stride) * scale(axis, stride)
            owner = (digits[:, None] + owner[None, :]).reshape(-1)
    return owner


SEQ_X = (4, 1)
SEQ_Z = (2, 4)
SEQ_Y = (4, 8)


def layer_norm(values):
    row_mean = jnp.mean(values, axis=-1, keepdims=True)
    centred = values - row_mean
    row_var = jnp.mean(centred * centred, axis=-1, keepdims=True)
    return centred / jnp.sqrt(row_var + 1e-06)


def attention_kernel(*refs, masked, carry, final):
    count = len(masked)
    q_ref = refs[0]
    key_refs = refs[1 : 1 + 2 * count : 2]
    value_refs = refs[2 : 2 + 2 * count : 2]
    rest = list(refs[1 + 2 * count :])
    masks = [rest.pop(0)[...] > 0.0 if m else None for m in masked]
    if carry:
        top_in, total_in, mixed_in = rest[0][...], rest[1][...], rest[2][...]
        rest = rest[3:]
    contract = (((1,), (1,)), ((), ()))
    tops, totals, mixes = [], [], []
    for head in range(q_ref.shape[1] // HEAD_DIM):
        lanes = slice(head * HEAD_DIM, (head + 1) * HEAD_DIM)
        query = q_ref[:, lanes]
        parts = []
        for k_ref, usable in zip(key_refs, masks):
            part = (
                lax.dot_general(query, k_ref[:, lanes], contract, preferred_element_type=jnp.float32)
                * 0.125
            )
            parts.append(part if usable is None else jnp.where(usable, part, -1e30))
        top = jnp.max(parts[0], axis=-1, keepdims=True)
        for part in parts[1:]:
            top = jnp.maximum(top, jnp.max(part, axis=-1, keepdims=True))
        if carry:
            old_top = top_in[:, head * HEAD_DIM : head * HEAD_DIM + 1]
            top = jnp.maximum(top, old_top)
            scale = jnp.exp(old_top - top)
            total = total_in[:, head * HEAD_DIM : head * HEAD_DIM + 1] * scale
            mixed = mixed_in[:, lanes] * scale
        else:
            total = jnp.zeros((query.shape[0], 1), jnp.float32)
            mixed = jnp.zeros((query.shape[0], HEAD_DIM), jnp.float32)
        for part, v_ref in zip(parts, value_refs):
            probs = jnp.exp(part - top)
            total = total + jnp.sum(probs, axis=-1, keepdims=True)
            mixed = mixed + jnp.dot(
                probs.astype(jnp.bfloat16), v_ref[:, lanes], preferred_element_type=jnp.float32
            )
        tops.append(jnp.broadcast_to(top, mixed.shape))
        totals.append(jnp.broadcast_to(total, mixed.shape))
        mixes.append(mixed)
    if final:
        o_ref = rest[0]
        o_ref[...] = jnp.concatenate(
            [m / t for m, t in zip(mixes, totals)], axis=1
        ).astype(o_ref.dtype)
    else:
        rest[0][...] = jnp.concatenate(tops, axis=1)
        rest[1][...] = jnp.concatenate(totals, axis=1)
        rest[2][...] = jnp.concatenate(mixes, axis=1)


def attention(image_qkv, pieces, masks, state=None, final=True):
    rows = image_qkv.shape[0]
    pairs = HEADS // 4
    width = 4 * HEAD_DIM
    heads_width = HEADS * HEAD_DIM

    def spec(array, offset):
        return pl.BlockSpec((array.shape[0], width), lambda j: (0, j + offset))

    operands = [image_qkv]
    in_specs = [spec(image_qkv, 0)]
    for piece in pieces:
        operands += [piece, piece]
        in_specs += [spec(piece, 0), spec(piece, pairs)]
    for mask in masks:
        if mask is not None:
            operands.append(mask)
            in_specs.append(pl.BlockSpec(mask.shape, lambda j: (0, 0)))
    if state is not None:
        operands += list(state)
        in_specs += [spec(part, 0) for part in state]
    out_spec = pl.BlockSpec((rows, width), lambda j: (0, j))
    if final:
        out_specs = out_spec
        out_shape = jax.ShapeDtypeStruct((rows, heads_width), jnp.bfloat16)
    else:
        out_specs = [out_spec] * 3
        out_shape = [jax.ShapeDtypeStruct((rows, heads_width), jnp.float32)] * 3
    kernel = functools.partial(
        attention_kernel,
        masked=tuple(m is not None for m in masks),
        carry=state is not None,
        final=final,
    )
    return pl.pallas_call(
        kernel, grid=(pairs,), in_specs=in_specs, out_specs=out_specs, out_shape=out_shape
    )(*operands)


def reorder(values, cols):
    picks = jnp.arange(values.shape[1], dtype=jnp.int32)[:, None] == cols[None, :]
    return jnp.dot(values, picks.astype(values.dtype), preferred_element_type=jnp.float32).astype(
        values.dtype
    )


def per_device(
    image_tokens,
    text_tokens,
    mod_image,
    mod_text,
    text_lengths,
    item_group,
    item_step,
    step_sizes,
    guide_scales,
    qkv_weight,
    kv_weight,
    out_weight,
):
    image_rows = image_tokens.shape[1]
    text_rows = text_tokens.shape[2]
    model_width = image_tokens.shape[2]
    heads_width = HEADS * HEAD_DIM
    picture = image_tokens[0]
    mod_one = mod_image[0, 0]
    mod_two = mod_text[0, 0]

    rep_size = lax.axis_size("rep")
    seq_size = lax.axis_size("seq")
    piece_rows = qkv_weight.shape[0]
    rep_route = ("rep", rep_size, 1, False)
    z_route = ("seq", *SEQ_Z)
    route_a = (rep_route, z_route, None, ("seq", *SEQ_X, False), ("seq", *SEQ_Y))
    route_b = (rep_route, z_route, None, ("seq", *SEQ_Y, False), ("seq", *SEQ_X))
    qkv_cols = qkv_weight.shape[1]
    (packed,) = staged_gather(
        (jnp.concatenate([qkv_weight, kv_weight, out_weight.reshape(piece_rows, -1)], axis=1),),
        (route_a[:3],),
    )
    qkv_half, rest_half = staged_gather(
        (packed[:, :qkv_cols], packed[:, qkv_cols:]), (route_a[3:], route_b[3:])
    )
    qkv_half = qkv_half.reshape(-1, qkv_half.shape[-1])
    rest_half = rest_half.reshape(-1, rest_half.shape[-1])
    kv_cols = kv_weight.shape[1]
    kv_half = rest_half[:, :kv_cols]
    out_half = rest_half[:, kv_cols:].reshape(-1, out_weight.shape[1])
    cfg_index = lax.axis_index("cfg")

    def weight_scale(axis, stride):
        return stride * rep_size if axis == "seq" else stride

    source_a = route_owner(route_a, weight_scale)
    source_b = route_owner(route_b, weight_scale)

    def columns(half, rows, source):
        owner = half * (seq_size * rep_size) + source
        return (owner[:, None] * rows + jnp.arange(rows, dtype=jnp.int32)[None, :]).reshape(-1)

    own_text = text_tokens[0, 0].astype(jnp.float32)
    swapped = partner_2(jnp.concatenate([mod_one, own_text, mod_two]), "cfg", 0)
    mod_other = swapped[: mod_one.shape[0]]
    text_other = swapped[mod_one.shape[0] : mod_one.shape[0] + own_text.shape[0]]
    mod_text_other = swapped[mod_one.shape[0] + own_text.shape[0] :]

    def modulate(values, mod):
        return (layer_norm(values.astype(jnp.float32)) * (1.0 + mod[1]) + mod[0]).astype(
            jnp.bfloat16
        )

    image_mod = modulate(picture, mod_one)
    text_mod = modulate(text_tokens[0, 0], mod_two)
    image_other = modulate(picture, mod_other)
    text_other_mod = modulate(text_other, mod_text_other)
    cols_a = columns(cfg_index, piece_rows, source_a)
    cols_b = columns(cfg_index, piece_rows, source_b)

    def project(values, weight, cols):
        return jnp.dot(reorder(values, cols), weight, preferred_element_type=jnp.float32)

    image_reordered = reorder(image_other, cols_a)
    key_value_cols = qkv_half[:, heads_width:]
    sent = partner_2(
        (
            jnp.dot(image_reordered, key_value_cols, preferred_element_type=jnp.float32),
            project(text_other_mod, kv_half, cols_b),
        ),
        "cfg",
        0,
    )
    sent_query = partner_2(
        jnp.dot(image_reordered, qkv_half[:, :heads_width], preferred_element_type=jnp.float32),
        "cfg",
        0,
    )
    own_reordered = reorder(image_mod, cols_a)
    key_value_total = (
        jnp.dot(own_reordered, key_value_cols, preferred_element_type=jnp.float32) + sent[0]
    )
    query_total = (
        jnp.dot(own_reordered, qkv_half[:, :heads_width], preferred_element_type=jnp.float32)
        + sent_query
    )
    kv_total = project(text_mod, kv_half, cols_b) + sent[1]
    out_other = partner_2(out_half, "cfg", 0)
    image_qkv = query_total.astype(jnp.bfloat16)
    text_kv = kv_total.astype(jnp.bfloat16)
    length = text_lengths[0, 0]
    image_kv = key_value_total.astype(jnp.bfloat16)

    cut = 64
    filler = (-(cut + text_rows)) % 16
    local = jnp.concatenate(
        [image_kv[:cut], text_kv, jnp.zeros((filler, image_kv.shape[1]), image_kv.dtype), image_kv[cut:]]
    )
    kv_route_a = (("seq", *SEQ_Z), ("seq", *SEQ_X), ("seq", *SEQ_Y))
    kv_route_b = (("seq", *SEQ_Z), ("seq", *SEQ_Y), ("seq", *SEQ_X))
    (local,) = staged_gather((local,), (kv_route_a[:1],))
    split = cut + text_rows + filler
    part_a, part_b = staged_gather(
        (local[:, :split], local[:, split:]), (kv_route_a[1:2], kv_route_b[1:2])
    )
    left_a, right_a = ring_neighbours(part_a, "seq", *SEQ_Y)
    left_b, right_b = ring_neighbours(part_b, "seq", *SEQ_X)
    owners = piece_owners(
        route_owner(kv_route_a[:2], lambda axis, stride: stride),
        slot_digits("seq", *SEQ_Y) * SEQ_Y[1],
    )
    row = jnp.arange(split, dtype=jnp.int32)[None, :]
    width = image_kv.shape[1]
    masks = []
    for owner in owners:
        position = owner[:, None] * text_rows + row - cut
        valid = (row < cut) | ((row < cut + text_rows) & (position < length))
        masks.append(valid.astype(jnp.float32).reshape(1, -1))
    def flat(p):
        return p.reshape(-1, width)

    state = attention(image_qkv, [flat(part_a), flat(part_b)], [masks[0], None], final=False)
    state, left_a, right_a, left_b, right_b = lax.optimization_barrier(
        (state, left_a, right_a, left_b, right_b)
    )
    head_a, tail_a = ring_forward(left_a, right_a, "seq", *SEQ_Y)
    head_b, tail_b = ring_forward(left_b, right_b, "seq", *SEQ_X)
    state = attention(
        image_qkv,
        [flat(right_a), flat(left_a), flat(right_b), flat(left_b)],
        [masks[1], masks[4], None, None],
        state,
        final=False,
    )
    attended = attention(
        image_qkv,
        [flat(head_a), flat(tail_a), flat(head_b), flat(tail_b)],
        [masks[2], masks[3], None, None],
        state,
    )
    out_rows = out_weight.shape[0]
    projected = jnp.dot(
        reorder(attended, columns(cfg_index, out_rows, source_b)),
        out_half,
        preferred_element_type=jnp.float32,
    ) + jnp.dot(
        reorder(attended, columns(1 - cfg_index, out_rows, source_b)),
        out_other,
        preferred_element_type=jnp.float32,
    )
    velocity = mod_one[2] * projected
    half_width = model_width // 2
    guide_scale = jnp.sum(
        jnp.where(
            jnp.arange(guide_scales.shape[0], dtype=jnp.int32) == item_group[0], guide_scales, 0.0
        )
    )
    step_size = jnp.sum(
        jnp.where(jnp.arange(step_sizes.shape[0], dtype=jnp.int32) == item_step[0], step_sizes, 0.0)
    )
    partner = partner_2(velocity.astype(jnp.bfloat16), "cfg", 0).astype(velocity.dtype)
    cond_full = jnp.where(cfg_index == 0, velocity, partner)
    uncond_full = jnp.where(cfg_index == 0, partner, velocity)
    conditional = lax.dynamic_slice_in_dim(cond_full, cfg_index * half_width, half_width, 1)
    unconditional = lax.dynamic_slice_in_dim(uncond_full, cfg_index * half_width, half_width, 1)
    guided = unconditional + guide_scale * (conditional - unconditional)
    base_part = lax.dynamic_slice_in_dim(picture, cfg_index * half_width, half_width, 1)
    return (base_part + step_size * guided)[None]


def solution(mesh):
    placed = (
        P("rep", "seq", None),
        P("cfg", "rep", "seq", None),
        P("cfg", "rep", None, None),
        P("cfg", "rep", None, None),
        P("cfg", "rep"),
        P("rep"),
        P("rep"),
        P(),
        P(),
        P(("cfg", "seq", "rep"), None),
        P(("cfg", "seq", "rep"), None),
        P(("cfg", "seq", "rep"), None),
    )
    return jax.shard_map(
        per_device, mesh=mesh, in_specs=placed, out_specs=P("rep", "seq", "cfg"), check_vma=False
    )
```
